128 devices in a mesh: adapter: 32 (over z, y, x_hi), tensor: 4 (over x_lo, core).
Axes of the slice: x: 4 (x_hi: 2, x_lo: 2; x = x_hi * 2 + x_lo), y: 4, z: 4, core: 2. Of those that a mesh axis runs over, the one named last changes fastest.
Arguments:
- partials: bfloat16 [4, 2048, 8192], P('tensor', 'adapter'), may hold values from -4 to 4
- residual: bfloat16 [2048, 8192], P('adapter'), may hold values from -80 to 80
- attention_norm_gain: bfloat16 [8192], replicated, may hold values from 0.25 to 1.75
- key_value_weight: bfloat16 [8192, 8, 256], P(None, 'tensor'), may hold values from -0.0625 to 0.0625
- adapter_down_weight: bfloat16 [8192, 32768], P('tensor', 'adapter'), may hold values from -0.0625 to 0.0625
- adapter_up_weight: bfloat16 [32768, 8, 256], P('adapter', 'tensor'), may hold values from -0.75 to 0.75
- row_adapter_index: int32 [2048], P('adapter'), may hold values from 0 to 511, as said below
- queries: bfloat16 [2048, 8192], P('adapter', 'tensor'), may hold values from -10 to 10
- key_value_cache: bfloat16 [256, 2, 1024, 1024], P('adapter', None, None, 'tensor'), may hold values from -10 to 10
- prompt_cache_length: int32 [256], P('adapter'), may hold values from 2 to 1024
Outputs:
- hidden_out: bfloat16 [2048, 8192], P('adapter', 'tensor')
- new_kv: bfloat16 [2048, 8, 256], P('adapter', 'tensor')
- attn_out: bfloat16 [2048, 8192], P('adapter', 'tensor')
The draws below stay inside these ranges and needn't reach their ends.
Inputs may be any that keep to these rules, and one draw needn't show every extreme that they name: `row_adapter_index`: adapter g is held by index g // 16 of the adapter axis. Of the 64 rows on one index of the adapter axis at most 8 use adapters held by one index; in every draw one index receives exactly 8 rows from every index.
All inputs are finite; a program needn't handle non-finite values.
Results may differ from the reference program's by a relative error of at most 0.012.
Values may be sent and summed in bfloat16 or wider, within the bound.
No kernel may reach another device: no remote copies, remote signals or barrier semaphores. Data moves between devices by JAX's collectives and lax.ppermute only.
A program may use at most 128 MiB of HBM per device.

```python
import math
import jax
import jax.numpy as jnp
from jax import lax

MODEL_DIM = 8192
HEADS = 64
KEY_VALUE_HEADS = 8
HEAD_SIZE = 128
ADAPTER_RANK = 64
FAN = 8
CACHE = 1024
ADAPT_DEV = 16
ROW_DEV = 64
PROMPTS = 256
ROWS = 2048
ADAPTER_TOTAL = 512
CAP = 8
N_TENSOR = 4


def draw_residual(key, part):
    noise_key, row_key, column_key = jax.random.split(key, 3)
    noise_draw = jnp.clip(jax.random.normal(noise_key, (ROWS, MODEL_DIM), jnp.float32), -4.0, 4.0)
    row_scale = jnp.exp(jax.random.uniform(row_key, (ROWS, 1), jnp.float32, math.log(0.25), math.log(2.5)))
    column_scale = jnp.exp(jax.random.uniform(column_key, (1, MODEL_DIM), jnp.float32, math.log(0.25), math.log(2.5)))
    position = jnp.arange(MODEL_DIM, dtype=jnp.float32)[None, :] / MODEL_DIM
    rise_factor = jnp.sqrt(1.0 + 6.0 * position)
    values = noise_draw * row_scale * column_scale * rise_factor
    return values.astype(jnp.bfloat16)


def draw_queries(key, part):
    draw_key = jax.random.fold_in(key, 1)
    values = jnp.clip(jax.random.normal(draw_key, (ROWS, HEADS * HEAD_SIZE), jnp.float32), -6.0, 6.0)
    return values.astype(jnp.bfloat16)


def draw_key_value_cache(key, part):
    draw_key = jax.random.fold_in(key, 2)
    shape_full = (PROMPTS, 2, CACHE, KEY_VALUE_HEADS * HEAD_SIZE)
    values = jnp.clip(jax.random.normal(draw_key, shape_full, jnp.float32), -6.0, 6.0)
    return values.astype(jnp.bfloat16)


def draw_row_adapter_index(key, part):
    owners = ADAPTER_TOTAL // ADAPT_DEV
    hot_key, perm_key, local_key = jax.random.split(key, 3)
    hot_owner = jax.random.randint(hot_key, (), 0, owners)
    candidates = (owners - 1) * CAP

    def one_block(block_key):
        choose_key, shuffle_key = jax.random.split(block_key)
        chosen = jax.random.permutation(choose_key, candidates)[:ROW_DEV - CAP]
        others = (chosen // CAP).astype(jnp.int32)
        others = others + (others >= hot_owner).astype(jnp.int32)
        owner_list = jnp.concatenate([jnp.full((CAP,), hot_owner, jnp.int32), others])
        return jax.random.permutation(shuffle_key, owner_list)
    owner_rows = jax.vmap(one_block)(jax.random.split(perm_key, owners)).reshape(ROWS)
    local_pick = jax.random.randint(local_key, (ROWS,), 0, ADAPT_DEV)
    return (owner_rows * ADAPT_DEV + local_pick).astype(jnp.int32)


def draw_prompt_cache_length(key, part):
    first_key, second_key, full_key = jax.random.split(key, 3)
    first_draw = jax.random.randint(first_key, (PROMPTS,), 0, CACHE - 1)
    second_draw = jax.random.randint(second_key, (PROMPTS,), 1, CACHE + 1)
    lengths = 2 + first_draw * second_draw // CACHE
    full_prompt = jax.random.randint(full_key, (), 0, PROMPTS)
    lengths = jnp.where(jnp.arange(PROMPTS) == full_prompt, CACHE, lengths)
    return lengths.astype(jnp.int32)


def block_levels(stream_key, extent, shards, smallest, largest):
    factor_of, own = 1.0, jax.random.fold_in(stream_key, 6)
    for dim, parts in shards:
        heights = jnp.exp(jax.random.uniform(jax.random.fold_in(own, dim), (parts,), jnp.float32, smallest / len(shards), largest / len(shards)))
        factor_of = factor_of * jnp.repeat(heights, extent[dim] // parts).reshape([-1 if axis == dim else 1 for axis in range(len(extent))])
    return factor_of


def normal_values(stream_key, dims, deviation, reach, cuts=(), kind=jnp.bfloat16):
    array = jax.random.normal(stream_key, dims, jnp.float32) * deviation
    if len(cuts) > 0:
        array = block_levels(stream_key, dims, cuts, -0.22, 0.18) * array
    return jnp.clip(array, min=-reach, max=reach).astype(kind)


def setup_inputs(seed: int = 0) -> dict:
    splits = jax.random.split(jax.random.key(seed), 11)
    partials = normal_values(splits[0], (N_TENSOR, ROWS, MODEL_DIM), 0.3, 4.0, ((0, 4), (1, 32)))
    residual = draw_residual(jax.random.fold_in(splits[10], 71), 0)
    attention_norm_gain = jnp.clip(1.0 + 0.15 * jax.random.normal(splits[2], (MODEL_DIM,), jnp.float32), 0.25, 1.75).astype(jnp.bfloat16)
    key_value_weight = normal_values(splits[3], (MODEL_DIM, KEY_VALUE_HEADS, 2 * HEAD_SIZE), MODEL_DIM ** -0.5, 0.0625, ((1, 4),))
    adapter_down_weight = normal_values(splits[4], (MODEL_DIM, ADAPTER_TOTAL * ADAPTER_RANK), MODEL_DIM ** -0.5, 0.0625, ((0, 4), (1, 32)))
    adapter_up_weight = normal_values(splits[5], (ADAPTER_TOTAL * ADAPTER_RANK, KEY_VALUE_HEADS, 2 * HEAD_SIZE), ADAPTER_RANK ** -0.5, 0.75, ((0, 32), (1, 4)))
    row_adapter_index = draw_row_adapter_index(jax.random.fold_in(splits[10], 71), 0)
    queries = draw_queries(jax.random.fold_in(splits[10], 71), 0)
    key_value_cache = draw_key_value_cache(jax.random.fold_in(splits[10], 71), 0)
    prompt_cache_length = draw_prompt_cache_length(jax.random.fold_in(splits[10], 71), 0)
    return {"partials": partials, "residual": residual, "attention_norm_gain": attention_norm_gain, "key_value_weight": key_value_weight, "adapter_down_weight": adapter_down_weight, "adapter_up_weight": adapter_up_weight, "row_adapter_index": row_adapter_index, "queries": queries, "key_value_cache": key_value_cache, "prompt_cache_length": prompt_cache_length}


EPSILON = 1e-05
ADAPTER_SCALE = 0.5

def reference(partials, residual, attention_norm_gain, key_value_weight, adapter_down_weight, adapter_up_weight, row_adapter_index, queries, key_value_cache, prompt_cache_length):
    summed = residual.astype(jnp.float32) + lax.optimization_barrier(jnp.sum(partials.astype(jnp.float32), axis=0))
    hidden_out = summed.astype(jnp.bfloat16)
    hidden_wide = hidden_out.astype(jnp.float32)
    mean_sq = lax.optimization_barrier(jnp.mean(hidden_wide * hidden_wide, axis=1, keepdims=True))
    normalized_input = (hidden_wide * lax.rsqrt(mean_sq + EPSILON) * attention_norm_gain.astype(jnp.float32)).astype(jnp.bfloat16)
    key_value_width = KEY_VALUE_HEADS * 2 * HEAD_SIZE
    base_kv = jnp.dot(normalized_input, key_value_weight.reshape(MODEL_DIM, key_value_width), preferred_element_type=jnp.float32)
    flattened_up = adapter_up_weight.reshape(ADAPTER_TOTAL * ADAPTER_RANK, key_value_width)

    def adapter_row(prompt_entry):
        normed_row, adapter_id = prompt_entry
        offset_index = (adapter_id * ADAPTER_RANK).astype(jnp.int32)
        down_weight_block = lax.dynamic_slice_in_dim(adapter_down_weight, offset_index, ADAPTER_RANK, 1)
        reduced_rank_rows = jnp.dot(normed_row[None, :], down_weight_block, preferred_element_type=jnp.float32).astype(jnp.bfloat16)
        up_weight_block = lax.dynamic_slice_in_dim(flattened_up, offset_index, ADAPTER_RANK, 0)
        return (ADAPTER_SCALE * jnp.dot(reduced_rank_rows, up_weight_block, preferred_element_type=jnp.float32)).astype(jnp.bfloat16)[0]
    update_rows = lax.map(adapter_row, (normalized_input, row_adapter_index))
    new_kv = (base_kv + update_rows.astype(jnp.float32)).astype(jnp.bfloat16).reshape(ROWS, KEY_VALUE_HEADS, 2 * HEAD_SIZE)
    group_size = HEADS // KEY_VALUE_HEADS
    score_scale = HEAD_SIZE ** (-0.5)
    query_heads = queries.reshape(PROMPTS, FAN, KEY_VALUE_HEADS, group_size, HEAD_SIZE)
    new_heads = new_kv.reshape(PROMPTS, FAN, KEY_VALUE_HEADS, 2 * HEAD_SIZE)
    cache_heads = key_value_cache.reshape(PROMPTS, 2, CACHE, KEY_VALUE_HEADS, HEAD_SIZE)

    def attend_prompt(prompt_entry):
        query_block, cache_block, length, new_block = prompt_entry
        query_wide = query_block.astype(jnp.float32)
        cache_keys = cache_block[0].astype(jnp.float32)
        cache_values = cache_block[1].astype(jnp.float32)
        scores = jnp.einsum('fkgd,ckd->fkgc', query_wide, cache_keys) * score_scale
        valid_mask = jnp.arange(CACHE) < length
        scores = jnp.where(valid_mask, scores, -jnp.inf)
        own_key = new_block[:, :, :HEAD_SIZE].astype(jnp.float32)
        own_value = new_block[:, :, HEAD_SIZE:].astype(jnp.float32)
        own_score = jnp.einsum('fkgd,fkd->fkg', query_wide, own_key) * score_scale
        score_top = jnp.maximum(lax.optimization_barrier(jnp.max(scores, axis=-1)), own_score)
        weights_low = jnp.exp(scores - score_top[:, :, :, None]).astype(jnp.bfloat16)
        weights = lax.optimization_barrier(weights_low).astype(jnp.float32)
        own_low = jnp.exp(own_score - score_top).astype(jnp.bfloat16)
        own_weight = lax.optimization_barrier(own_low).astype(jnp.float32)
        weight_total = lax.optimization_barrier(jnp.sum(weights, axis=-1)) + own_weight
        weighted = jnp.einsum('fkgc,ckd->fkgd', weights, cache_values) + own_weight[:, :, :, None] * own_value[:, :, None, :]
        return (weighted / weight_total[:, :, :, None]).astype(jnp.bfloat16)
    attended = lax.map(attend_prompt, (query_heads, cache_heads, prompt_cache_length, new_heads))
    attn_out = attended.reshape(ROWS, HEADS * HEAD_SIZE)
    return (hidden_out, new_kv, attn_out)
```

```python
import jax
import jax.numpy as jnp
from jax import lax
from jax.sharding import PartitionSpec as P

HEAD_SIZE = 128
ADAPTER_RANK = 64
FAN = 8


EPSILON = 1e-05
ADAPTER_SCALE = 0.5
ID_LANES = 128


def _swap(x, mask, count):
    return lax.ppermute(x, "tensor", perm=[(i, i ^ mask) for i in range(count)])


def per_device(
    partials,
    residual,
    attention_norm_gain,
    key_value_weight,
    adapter_down_weight,
    adapter_up_weight,
    row_adapter_index,
    queries,
    key_value_cache,
    prompt_cache_length,
):
    row_dev = residual.shape[0]
    model_width = residual.shape[1]
    tensor_count = lax.axis_size("tensor")
    quarter = model_width // tensor_count
    tensor_index = lax.axis_index("tensor")
    core = tensor_index % 2
    chip_x = tensor_index // 2
    flat_weight = key_value_weight.reshape(model_width, -1)

    part4 = partials[0].reshape(row_dev, 2, 2, quarter)
    res4 = residual.reshape(row_dev, 2, 2, quarter)
    mine_p = lax.dynamic_index_in_dim(part4, core, axis=2, keepdims=False)
    other_p = lax.dynamic_index_in_dim(part4, 1 - core, axis=2, keepdims=False)
    got_p = _swap(other_p, 1, tensor_count)
    chip_sum = mine_p.astype(jnp.float32) + got_p.astype(jnp.float32)
    far_sum = _swap(chip_sum.astype(jnp.bfloat16), 2, tensor_count)
    res_half = lax.dynamic_index_in_dim(res4, core, axis=2, keepdims=False)
    hidden_half = (
        res_half.astype(jnp.float32) + (chip_sum + far_sum.astype(jnp.float32))
    ).astype(jnp.bfloat16)
    hidden_part = lax.dynamic_index_in_dim(hidden_half, chip_x, axis=1, keepdims=False)
    hidden_other = _swap(hidden_half, 1, tensor_count)
    first = core == 0
    half0 = jnp.where(first, hidden_half, hidden_other)
    half1 = jnp.where(first, hidden_other, hidden_half)
    hidden_full = jnp.stack([half0, half1], axis=2).reshape(row_dev, model_width)

    hidden_wide = hidden_full.astype(jnp.float32)
    mean_sq = jnp.mean(hidden_wide * hidden_wide, axis=1, keepdims=True)
    normed_full = (
        hidden_wide * lax.rsqrt(mean_sq + EPSILON) * attention_norm_gain.astype(jnp.float32)
    ).astype(jnp.bfloat16)
    normed_part = lax.dynamic_slice_in_dim(normed_full, tensor_index * quarter, quarter, 1)
    base_kv = jnp.dot(normed_full, flat_weight, preferred_element_type=jnp.float32)

    adapt_count = lax.axis_size("adapter")
    capacity = max(2, 4 * row_dev // adapt_count)
    slot_count = adapt_count * capacity
    adapter_grouped = adapter_down_weight.shape[1] // ADAPTER_RANK
    owner_index = row_adapter_index // adapter_grouped
    local_id = row_adapter_index % adapter_grouped
    row_order = jnp.arange(row_dev)
    same_owner = owner_index[:, None] == owner_index[None, :]
    earlier = row_order[None, :] < row_order[:, None]
    slot_rank = jnp.sum((same_owner & earlier).astype(jnp.int32), axis=1)
    row_slot = owner_index * capacity + slot_rank
    row_to_slot = jnp.arange(slot_count)[:, None] == row_slot[None, :]
    slot_matrix = row_to_slot.astype(jnp.bfloat16)
    send_rows = jnp.dot(slot_matrix, normed_part, preferred_element_type=jnp.float32).astype(
        jnp.bfloat16
    )
    send_ids = jnp.sum(jnp.where(row_to_slot, local_id[None, :] + 1, 0), axis=1) - 1
    id_block = jnp.broadcast_to(send_ids.astype(jnp.bfloat16)[:, None], (slot_count, ID_LANES))
    payload = jnp.concatenate([send_rows, id_block], axis=1).reshape(
        adapt_count, capacity, quarter + ID_LANES
    )
    flattened_up = adapter_up_weight.reshape(adapter_grouped * ADAPTER_RANK, -1)
    rows_in = lax.all_to_all(payload, "adapter", split_axis=0, concat_axis=0, tiled=True)
    item_count = rows_in.shape[1]
    rows_in = rows_in.reshape(slot_count, quarter + ID_LANES)
    flattened_rows = rows_in[:, :quarter]
    ids_in = rows_in[:, quarter].astype(jnp.int32)
    adapter_pick = ids_in[:, None] == jnp.arange(adapter_grouped)[None, :]
    projected_rows = jnp.dot(
        flattened_rows, adapter_down_weight, preferred_element_type=jnp.float32
    ).reshape(-1, adapter_grouped, ADAPTER_RANK)
    partial_low = jnp.sum(jnp.where(adapter_pick[:, :, None], projected_rows, 0.0), axis=1)
    pair_low = partial_low + _swap(partial_low, 1, tensor_count)
    reduced_rank_rows = (pair_low + _swap(pair_low, 2, tensor_count)).astype(jnp.bfloat16)
    expanded_rows = jnp.where(
        adapter_pick[:, :, None], reduced_rank_rows[:, None, :], jnp.zeros((), jnp.bfloat16)
    ).reshape(-1, adapter_grouped * ADAPTER_RANK)
    adapter_update = (
        ADAPTER_SCALE * jnp.dot(expanded_rows, flattened_up, preferred_element_type=jnp.float32)
    ).astype(jnp.bfloat16)
    adapter_update = adapter_update.reshape(adapt_count, item_count, -1)
    returned = lax.all_to_all(adapter_update, "adapter", split_axis=0, concat_axis=0, tiled=True)
    returned = returned.reshape(slot_count, -1)
    update_rows = lax.dot_general(
        slot_matrix, returned, (((0,), (0,)), ((), ())), preferred_element_type=jnp.float32
    )
    local_heads = key_value_weight.shape[1]
    new_kv = (
        (base_kv + update_rows).astype(jnp.bfloat16).reshape(row_dev, local_heads, 2 * HEAD_SIZE)
    )

    local_prompts = key_value_cache.shape[0]
    cache_length = key_value_cache.shape[2]
    group_size = queries.shape[1] // (local_heads * HEAD_SIZE)
    score_scale = HEAD_SIZE ** (-0.5)
    query_heads = queries.reshape(local_prompts, FAN, local_heads, group_size, HEAD_SIZE)
    cache_keys = key_value_cache[:, 0].reshape(local_prompts, cache_length, local_heads, HEAD_SIZE)
    cache_values = key_value_cache[:, 1].reshape(
        local_prompts, cache_length, local_heads, HEAD_SIZE
    )
    scores = (
        jnp.einsum("pfkgd,pckd->pfkgc", query_heads, cache_keys, preferred_element_type=jnp.float32)
        * score_scale
    )
    valid_mask = jnp.arange(cache_length)[None, :] < prompt_cache_length[:, None]
    scores = jnp.where(valid_mask[:, None, None, None, :], scores, -jnp.inf)
    cache_top = jnp.max(scores, axis=-1)
    weights = jnp.exp(scores - cache_top[..., None]).astype(jnp.bfloat16)
    cache_total = jnp.sum(weights, axis=-1, dtype=jnp.float32)
    cache_weighted = jnp.einsum(
        "pfkgc,pckd->pfkgd", weights, cache_values, preferred_element_type=jnp.float32
    )

    new_heads = new_kv.reshape(local_prompts, FAN, local_heads, 2 * HEAD_SIZE)
    own_key = new_heads[:, :, :, :HEAD_SIZE]
    own_value = new_heads[:, :, :, HEAD_SIZE:]
    own_score = (
        jnp.einsum("pfkgd,pfkd->pfkg", query_heads, own_key, preferred_element_type=jnp.float32)
        * score_scale
    )
    score_top = jnp.maximum(cache_top, own_score)
    rescale = jnp.exp(cache_top - score_top)
    own_weight = jnp.exp(own_score - score_top).astype(jnp.bfloat16).astype(jnp.float32)
    weight_total = rescale * cache_total + own_weight
    weighted = (
        rescale[..., None] * cache_weighted
        + own_weight[..., None] * own_value.astype(jnp.float32)[:, :, :, None, :]
    )
    attended = (weighted / weight_total[..., None]).astype(jnp.bfloat16).reshape(row_dev, -1)
    return (hidden_part, new_kv, attended)


def solution(mesh):
    return jax.shard_map(
        per_device,
        mesh=mesh,
        in_specs=(
            P("tensor", "adapter", None),
            P("adapter", None),
            P(),
            P(None, "tensor", None),
            P("tensor", "adapter"),
            P("adapter", "tensor", None),
            P("adapter"),
            P("adapter", "tensor"),
            P("adapter", None, None, "tensor"),
            P("adapter"),
        ),
        out_specs=(P("adapter", "tensor"), P("adapter", "tensor", None), P("adapter", "tensor")),
        check_vma=False,
    )
```

```python
import jax
import jax.numpy as jnp
from jax import lax
from jax.sharding import PartitionSpec as P

HEAD_SIZE = 128
ADAPTER_RANK = 64
FAN = 8


EPSILON = 1e-05
ADAPTER_SCALE = 0.5
ID_LANES = 128


def _swap(x, mask, count):
    return lax.ppermute(x, "tensor", perm=[(i, i ^ mask) for i in range(count)])


def _shift(x, step, count):
    return lax.ppermute(x, "adapter", perm=[(i, (i + step) % count) for i in range(count)])


def per_device(
    partials,
    residual,
    attention_norm_gain,
    key_value_weight,
    adapter_down_weight,
    adapter_up_weight,
    row_adapter_index,
    queries,
    key_value_cache,
    prompt_cache_length,
):
    row_dev = residual.shape[0]
    model_width = residual.shape[1]
    tensor_count = lax.axis_size("tensor")
    quarter = model_width // tensor_count
    tensor_index = lax.axis_index("tensor")
    core = tensor_index % 2
    chip_x = tensor_index // 2
    flat_weight = key_value_weight.reshape(model_width, -1)

    part4 = partials[0].reshape(row_dev, 2, 2, quarter)
    res4 = residual.reshape(row_dev, 2, 2, quarter)
    mine_p = lax.dynamic_index_in_dim(part4, core, axis=2, keepdims=False)
    other_p = lax.dynamic_index_in_dim(part4, 1 - core, axis=2, keepdims=False)
    got_p = _swap(other_p, 1, tensor_count)
    chip_sum = mine_p.astype(jnp.float32) + got_p.astype(jnp.float32)
    far_sum = _swap(chip_sum.astype(jnp.bfloat16), 2, tensor_count)
    res_half = lax.dynamic_index_in_dim(res4, core, axis=2, keepdims=False)
    hidden_half = (
        res_half.astype(jnp.float32) + (chip_sum + far_sum.astype(jnp.float32))
    ).astype(jnp.bfloat16)
    hidden_part = lax.dynamic_index_in_dim(hidden_half, chip_x, axis=1, keepdims=False)
    hidden_other = _swap(hidden_half, 1, tensor_count)
    first = core == 0
    half0 = jnp.where(first, hidden_half, hidden_other)
    half1 = jnp.where(first, hidden_other, hidden_half)
    hidden_full = jnp.stack([half0, half1], axis=2).reshape(row_dev, model_width)

    hidden_wide = hidden_full.astype(jnp.float32)
    mean_sq = jnp.mean(hidden_wide * hidden_wide, axis=1, keepdims=True)
    normed_full = (
        hidden_wide * lax.rsqrt(mean_sq + EPSILON) * attention_norm_gain.astype(jnp.float32)
    ).astype(jnp.bfloat16)
    normed_part = lax.dynamic_slice_in_dim(normed_full, tensor_index * quarter, quarter, 1)
    base_kv = jnp.dot(normed_full, flat_weight, preferred_element_type=jnp.float32)

    adapt_count = lax.axis_size("adapter")
    capacity = max(2, 4 * row_dev // adapt_count)
    slot_count = adapt_count * capacity
    adapter_grouped = adapter_down_weight.shape[1] // ADAPTER_RANK
    owner_index = row_adapter_index // adapter_grouped
    local_id = row_adapter_index % adapter_grouped
    my_adapter = lax.axis_index("adapter")
    shift_of_row = (owner_index - my_adapter) % adapt_count
    row_order = jnp.arange(row_dev)
    same_owner = owner_index[:, None] == owner_index[None, :]
    earlier = row_order[None, :] < row_order[:, None]
    slot_rank = jnp.sum((same_owner & earlier).astype(jnp.int32), axis=1)
    row_slot = shift_of_row * capacity + slot_rank
    row_to_slot = jnp.arange(slot_count)[:, None] == row_slot[None, :]
    slot_matrix = row_to_slot.astype(jnp.bfloat16)
    send_rows = jnp.dot(slot_matrix, normed_part, preferred_element_type=jnp.float32).astype(
        jnp.bfloat16
    )
    send_ids = jnp.sum(jnp.where(row_to_slot, local_id[None, :] + 1, 0), axis=1) - 1
    id_block = jnp.broadcast_to(send_ids.astype(jnp.bfloat16)[:, None], (slot_count, ID_LANES))
    payload = jnp.concatenate([send_rows, id_block], axis=1).reshape(
        adapt_count, capacity, quarter + ID_LANES
    )
    flattened_up = adapter_up_weight.reshape(adapter_grouped * ADAPTER_RANK, -1)
    rows_in = jnp.stack(
        [payload[0]]
        + [_shift(payload[s], s, adapt_count) for s in range(1, adapt_count)]
    )
    item_count = rows_in.shape[1]
    rows_in = rows_in.reshape(slot_count, quarter + ID_LANES)
    flattened_rows = rows_in[:, :quarter]
    ids_in = rows_in[:, quarter].astype(jnp.int32)
    adapter_pick = ids_in[:, None] == jnp.arange(adapter_grouped)[None, :]
    projected_rows = jnp.dot(
        flattened_rows, adapter_down_weight, preferred_element_type=jnp.float32
    ).reshape(-1, adapter_grouped, ADAPTER_RANK)
    partial_low = jnp.sum(jnp.where(adapter_pick[:, :, None], projected_rows, 0.0), axis=1)
    pair_low = partial_low + _swap(partial_low, 1, tensor_count)
    reduced_rank_rows = (pair_low + _swap(pair_low, 2, tensor_count)).astype(jnp.bfloat16)
    expanded_rows = jnp.where(
        adapter_pick[:, :, None], reduced_rank_rows[:, None, :], jnp.zeros((), jnp.bfloat16)
    ).reshape(-1, adapter_grouped * ADAPTER_RANK)
    adapter_update = (
        ADAPTER_SCALE * jnp.dot(expanded_rows, flattened_up, preferred_element_type=jnp.float32)
    ).astype(jnp.bfloat16)
    adapter_update = adapter_update.reshape(adapt_count, item_count, -1)
    returned = jnp.stack(
        [adapter_update[0]]
        + [_shift(adapter_update[s], -s, adapt_count) for s in range(1, adapt_count)]
    )
    returned = returned.reshape(slot_count, -1)
    update_rows = lax.dot_general(
        slot_matrix, returned, (((0,), (0,)), ((), ())), preferred_element_type=jnp.float32
    )
    local_heads = key_value_weight.shape[1]
    new_kv = (
        (base_kv + update_rows).astype(jnp.bfloat16).reshape(row_dev, local_heads, 2 * HEAD_SIZE)
    )

    local_prompts = key_value_cache.shape[0]
    cache_length = key_value_cache.shape[2]
    group_size = queries.shape[1] // (local_heads * HEAD_SIZE)
    score_scale = HEAD_SIZE ** (-0.5)
    query_heads = queries.reshape(local_prompts, FAN, local_heads, group_size, HEAD_SIZE)
    cache_keys = key_value_cache[:, 0].reshape(local_prompts, cache_length, local_heads, HEAD_SIZE)
    cache_values = key_value_cache[:, 1].reshape(
        local_prompts, cache_length, local_heads, HEAD_SIZE
    )
    scores = (
        jnp.einsum("pfkgd,pckd->pfkgc", query_heads, cache_keys, preferred_element_type=jnp.float32)
        * score_scale
    )
    valid_mask = jnp.arange(cache_length)[None, :] < prompt_cache_length[:, None]
    scores = jnp.where(valid_mask[:, None, None, None, :], scores, -jnp.inf)
    cache_top = jnp.max(scores, axis=-1)
    weights = jnp.exp(scores - cache_top[..., None]).astype(jnp.bfloat16)
    cache_total = jnp.sum(weights, axis=-1, dtype=jnp.float32)
    cache_weighted = jnp.einsum(
        "pfkgc,pckd->pfkgd", weights, cache_values, preferred_element_type=jnp.float32
    )
    cache_top, cache_total, cache_weighted = lax.optimization_barrier(
        (cache_top, cache_total, cache_weighted)
    )

    new_heads = new_kv.reshape(local_prompts, FAN, local_heads, 2 * HEAD_SIZE)
    own_key = new_heads[:, :, :, :HEAD_SIZE]
    own_value = new_heads[:, :, :, HEAD_SIZE:]
    own_score = (
        jnp.einsum("pfkgd,pfkd->pfkg", query_heads, own_key, preferred_element_type=jnp.float32)
        * score_scale
    )
    score_top = jnp.maximum(cache_top, own_score)
    rescale = jnp.exp(cache_top - score_top)
    own_weight = jnp.exp(own_score - score_top).astype(jnp.bfloat16).astype(jnp.float32)
    weight_total = rescale * cache_total + own_weight
    weighted = (
        rescale[..., None] * cache_weighted
        + own_weight[..., None] * own_value.astype(jnp.float32)[:, :, :, None, :]
    )
    attended = (weighted / weight_total[..., None]).astype(jnp.bfloat16).reshape(row_dev, -1)
    return (hidden_part, new_kv, attended)


def solution(mesh):
    return jax.shard_map(
        per_device,
        mesh=mesh,
        in_specs=(
            P("tensor", "adapter", None),
            P("adapter", None),
            P(),
            P(None, "tensor", None),
            P("tensor", "adapter"),
            P("adapter", "tensor", None),
            P("adapter"),
            P("adapter", "tensor"),
            P("adapter", None, None, "tensor"),
            P("adapter"),
        ),
        out_specs=(P("adapter", "tensor"), P("adapter", "tensor", None), P("adapter", "tensor")),
        check_vma=False,
    )
```

```python
import functools

import jax
import jax.numpy as jnp
from jax import lax
from jax.experimental import pallas as pl
from jax.experimental.pallas import tpu as pltpu
from jax.sharding import PartitionSpec as P

HEAD_SIZE = 128
ADAPTER_RANK = 64
FAN = 8


EPSILON = 1e-05
ADAPTER_SCALE = 0.5
ID_LANES = 128


def _attn_kernel(len_ref, q_ref, k_ref, v_ref, num_ref, top_ref, tot_ref, *, group, scale):
    p = pl.program_id(0)
    length = len_ref[p]
    q = q_ref[...]
    fan = q.shape[0]
    qs = jnp.concatenate([q[:, g * HEAD_SIZE:(g + 1) * HEAD_SIZE] for g in range(group)], axis=0)
    kb = k_ref[0, 0]
    s = lax.dot_general(qs, kb, (((1,), (1,)), ((), ())), preferred_element_type=jnp.float32) * scale
    col = lax.broadcasted_iota(jnp.int32, s.shape, 1)
    s = jnp.where(col < length, s, -jnp.inf)
    m = jnp.max(s, axis=1, keepdims=True)
    w = jnp.exp(s - m).astype(jnp.bfloat16)
    tot = jnp.sum(w.astype(jnp.float32), axis=1, keepdims=True)
    num = jnp.dot(w, v_ref[0, 0], preferred_element_type=jnp.float32)
    num_ref[...] = jnp.concatenate([num[g * fan:(g + 1) * fan] for g in range(group)], axis=1)
    top_ref[...] = jnp.concatenate(
        [jnp.broadcast_to(m[g * fan:(g + 1) * fan], (fan, HEAD_SIZE)) for g in range(group)], axis=1)
    tot_ref[...] = jnp.concatenate(
        [jnp.broadcast_to(tot[g * fan:(g + 1) * fan], (fan, HEAD_SIZE)) for g in range(group)], axis=1)


def cache_attention(queries, key_value_cache, prompt_cache_length, local_heads, fan):
    prompts, _, cache_len, _ = key_value_cache.shape
    rows, width = queries.shape
    head_width = width // local_heads
    group = head_width // HEAD_SIZE
    kernel = functools.partial(_attn_kernel, group=group, scale=HEAD_SIZE ** (-0.5))
    out = jax.ShapeDtypeStruct((rows, width), jnp.float32)
    spec_q = pl.BlockSpec((fan, head_width), lambda p, k, lens: (p, k))
    return pl.pallas_call(
        kernel,
        out_shape=(out, out, out),
        grid_spec=pltpu.PrefetchScalarGridSpec(
            num_scalar_prefetch=1,
            grid=(prompts, local_heads),
            in_specs=[
                spec_q,
                pl.BlockSpec((1, 1, cache_len, HEAD_SIZE), lambda p, k, lens: (p, 0, 0, k)),
                pl.BlockSpec((1, 1, cache_len, HEAD_SIZE), lambda p, k, lens: (p, 1, 0, k)),
            ],
            out_specs=[spec_q, spec_q, spec_q],
        ),
    )(prompt_cache_length, queries, key_value_cache, key_value_cache)


def _swap(x, mask, count):
    return lax.ppermute(x, "tensor", perm=[(i, i ^ mask) for i in range(count)])


def per_device(
    partials,
    residual,
    attention_norm_gain,
    key_value_weight,
    adapter_down_weight,
    adapter_up_weight,
    row_adapter_index,
    queries,
    key_value_cache,
    prompt_cache_length,
):
    row_dev = residual.shape[0]
    model_width = residual.shape[1]
    tensor_count = lax.axis_size("tensor")
    quarter = model_width // tensor_count
    tensor_index = lax.axis_index("tensor")
    core = tensor_index % 2
    chip_x = tensor_index // 2
    local_heads = key_value_weight.shape[1]
    head_weight = jnp.transpose(key_value_weight, (1, 0, 2))

    half_rows = row_dev // 2
    part2 = partials[0].reshape(2, half_rows, model_width)
    mine_p = lax.dynamic_index_in_dim(part2, core, axis=0, keepdims=False)
    other_p = lax.dynamic_index_in_dim(part2, 1 - core, axis=0, keepdims=False)
    got_p = _swap(other_p, 1, tensor_count)
    chip_sum = mine_p.astype(jnp.float32) + got_p.astype(jnp.float32)
    far_sum = _swap(chip_sum.astype(jnp.bfloat16), 2, tensor_count)
    attention_parts = cache_attention(
        queries, key_value_cache, prompt_cache_length, local_heads, FAN
    )
    far_sum, head_weight, attention_parts = lax.optimization_barrier(
        (far_sum, head_weight, attention_parts)
    )
    res_half = lax.dynamic_index_in_dim(
        residual.reshape(2, half_rows, model_width), core, axis=0, keepdims=False
    )
    hidden_half = (
        res_half.astype(jnp.float32) + (chip_sum + far_sum.astype(jnp.float32))
    ).astype(jnp.bfloat16)
    hidden_wide = hidden_half.astype(jnp.float32)
    mean_sq = jnp.mean(hidden_wide * hidden_wide, axis=1, keepdims=True)
    normed_half = (
        hidden_wide * lax.rsqrt(mean_sq + EPSILON) * attention_norm_gain.astype(jnp.float32)
    ).astype(jnp.bfloat16)
    partner_quarter = lax.dynamic_slice_in_dim(
        hidden_half, (tensor_index ^ 1) * quarter, quarter, 1
    )
    swap_in = _swap(jnp.concatenate([normed_half, partner_quarter], axis=1), 1, tensor_count)
    normed_other = swap_in[:, :model_width]
    hidden_other = swap_in[:, model_width:]
    hidden_mine = lax.dynamic_slice_in_dim(hidden_half, tensor_index * quarter, quarter, 1)
    first = core == 0
    hidden_part = jnp.where(
        first,
        jnp.concatenate([hidden_mine, hidden_other], axis=0),
        jnp.concatenate([hidden_other, hidden_mine], axis=0),
    )
    normed_full = jnp.where(
        first,
        jnp.concatenate([normed_half, normed_other], axis=0),
        jnp.concatenate([normed_other, normed_half], axis=0),
    )
    normed_part = lax.dynamic_slice_in_dim(normed_full, tensor_index * quarter, quarter, 1)
    base_kv = jnp.einsum(
        "rf,hfd->rhd", normed_full, head_weight, preferred_element_type=jnp.float32
    ).reshape(row_dev, -1)

    adapt_count = lax.axis_size("adapter")
    capacity = max(2, 4 * row_dev // adapt_count)
    slot_count = adapt_count * capacity
    adapter_grouped = adapter_down_weight.shape[1] // ADAPTER_RANK
    owner_index = row_adapter_index // adapter_grouped
    local_id = row_adapter_index % adapter_grouped
    row_order = jnp.arange(row_dev)
    same_owner = owner_index[:, None] == owner_index[None, :]
    earlier = row_order[None, :] < row_order[:, None]
    slot_rank = jnp.sum((same_owner & earlier).astype(jnp.int32), axis=1)
    row_slot = owner_index * capacity + slot_rank
    row_to_slot = jnp.arange(slot_count)[:, None] == row_slot[None, :]
    slot_matrix = row_to_slot.astype(jnp.bfloat16)
    send_rows = jnp.dot(slot_matrix, normed_part, preferred_element_type=jnp.float32).astype(
        jnp.bfloat16
    )
    send_ids = jnp.sum(jnp.where(row_to_slot, local_id[None, :] + 1, 0), axis=1) - 1
    id_block = jnp.broadcast_to(send_ids.astype(jnp.bfloat16)[:, None], (slot_count, ID_LANES))
    payload = jnp.concatenate([send_rows, id_block], axis=1).reshape(
        adapt_count, capacity, quarter + ID_LANES
    )
    flattened_up = adapter_up_weight.reshape(adapter_grouped * ADAPTER_RANK, -1)
    rows_in = lax.all_to_all(payload, "adapter", split_axis=0, concat_axis=0, tiled=True)
    item_count = rows_in.shape[1]
    rows_in = rows_in.reshape(slot_count, quarter + ID_LANES)
    flattened_rows = rows_in[:, :quarter]
    ids_in = rows_in[:, quarter].astype(jnp.int32)
    adapter_pick = ids_in[:, None] == jnp.arange(adapter_grouped)[None, :]
    projected_rows = jnp.dot(
        flattened_rows, adapter_down_weight, preferred_element_type=jnp.float32
    ).reshape(-1, adapter_grouped, ADAPTER_RANK)
    partial_low = jnp.sum(jnp.where(adapter_pick[:, :, None], projected_rows, 0.0), axis=1)
    pair_low = partial_low + _swap(partial_low, 1, tensor_count)
    far_low, base_kv = lax.optimization_barrier((_swap(pair_low, 2, tensor_count), base_kv))
    reduced_rank_rows = (pair_low + far_low).astype(jnp.bfloat16)
    expanded_rows = jnp.where(
        adapter_pick[:, :, None], reduced_rank_rows[:, None, :], jnp.zeros((), jnp.bfloat16)
    ).reshape(-1, adapter_grouped * ADAPTER_RANK)
    adapter_update = (
        ADAPTER_SCALE * jnp.dot(expanded_rows, flattened_up, preferred_element_type=jnp.float32)
    ).astype(jnp.bfloat16)
    adapter_update = adapter_update.reshape(adapt_count, item_count, -1)
    returned = lax.all_to_all(adapter_update, "adapter", split_axis=0, concat_axis=0, tiled=True)
    returned = returned.reshape(slot_count, -1)
    update_rows = lax.dot_general(
        slot_matrix, returned, (((0,), (0,)), ((), ())), preferred_element_type=jnp.float32
    )
    new_kv = (
        (base_kv + update_rows).astype(jnp.bfloat16).reshape(row_dev, local_heads, 2 * HEAD_SIZE)
    )

    local_prompts = key_value_cache.shape[0]
    group_size = queries.shape[1] // (local_heads * HEAD_SIZE)
    score_scale = HEAD_SIZE ** (-0.5)
    num_c, top_c, tot_c = attention_parts
    view = (row_dev, local_heads, group_size, HEAD_SIZE)
    cache_weighted = num_c.reshape(view)
    cache_top = top_c.reshape(view)[..., 0]
    cache_total = tot_c.reshape(view)[..., 0]
    query_heads = queries.reshape(view)
    own_key = new_kv[:, :, :HEAD_SIZE]
    own_value = new_kv[:, :, HEAD_SIZE:]
    own_score = (
        jnp.einsum("rkgd,rkd->rkg", query_heads, own_key, preferred_element_type=jnp.float32)
        * score_scale
    )
    score_top = jnp.maximum(cache_top, own_score)
    rescale = jnp.exp(cache_top - score_top)
    own_weight = jnp.exp(own_score - score_top).astype(jnp.bfloat16).astype(jnp.float32)
    weight_total = rescale * cache_total + own_weight
    weighted = (
        rescale[..., None] * cache_weighted
        + own_weight[..., None] * own_value.astype(jnp.float32)[:, :, None, :]
    )
    attended = (weighted / weight_total[..., None]).astype(jnp.bfloat16).reshape(row_dev, -1)
    return (hidden_part, new_kv, attended)


def solution(mesh):
    return jax.shard_map(
        per_device,
        mesh=mesh,
        in_specs=(
            P("tensor", "adapter", None),
            P("adapter", None),
            P(),
            P(None, "tensor", None),
            P("tensor", "adapter"),
            P("adapter", "tensor", None),
            P("adapter"),
            P("adapter", "tensor"),
            P("adapter", None, None, "tensor"),
            P("adapter"),
        ),
        out_specs=(P("adapter", "tensor"), P("adapter", "tensor", None), P("adapter", "tensor")),
        check_vma=False,
    )
```

```python
import functools

import jax
import jax.numpy as jnp
from jax import lax
from jax.experimental import pallas as pl
from jax.experimental.pallas import tpu as pltpu
from jax.sharding import PartitionSpec as P

HEAD_SIZE = 128
ADAPTER_RANK = 64
FAN = 8


EPSILON = 1e-05
ADAPTER_SCALE = 0.5
ID_LANES = 128


def _attn_kernel(len_ref, q_ref, k_ref, v_ref, num_ref, top_ref, tot_ref, *, heads, group, scale, first):
    p = pl.program_id(0) + first
    length = len_ref[p]
    fan = q_ref.shape[0]
    head_width = group * HEAD_SIZE
    for k in range(heads):
        lanes = pl.ds(k * HEAD_SIZE, HEAD_SIZE)
        qs = jnp.concatenate(
            [q_ref[:, pl.ds(k * head_width + g * HEAD_SIZE, HEAD_SIZE)] for g in range(group)], axis=0)
        kb = k_ref[0, 0, :, lanes]
        s = lax.dot_general(qs, kb, (((1,), (1,)), ((), ())), preferred_element_type=jnp.float32) * scale
        col = lax.broadcasted_iota(jnp.int32, s.shape, 1)
        s = jnp.where(col < length, s, -jnp.inf)
        m = jnp.max(s, axis=1, keepdims=True)
        w = jnp.exp(s - m).astype(jnp.bfloat16)
        tot = jnp.sum(w.astype(jnp.float32), axis=1, keepdims=True)
        num = jnp.dot(w, v_ref[0, 0, :, lanes], preferred_element_type=jnp.float32)
        for g in range(group):
            out_lanes = pl.ds(k * head_width + g * HEAD_SIZE, HEAD_SIZE)
            rows = slice(g * fan, (g + 1) * fan)
            num_ref[:, out_lanes] = num[rows]
            top_ref[:, out_lanes] = jnp.broadcast_to(m[rows], (fan, HEAD_SIZE))
            tot_ref[:, out_lanes] = jnp.broadcast_to(tot[rows], (fan, HEAD_SIZE))


def cache_attention(queries, key_value_cache, prompt_cache_length, local_heads, fan, first, count):
    _, _, cache_len, kv_width = key_value_cache.shape
    width = queries.shape[1]
    group = width // (local_heads * HEAD_SIZE)
    kernel = functools.partial(
        _attn_kernel, heads=local_heads, group=group, scale=HEAD_SIZE ** (-0.5), first=first)
    out = jax.ShapeDtypeStruct((count * fan, width), jnp.float32)
    spec_out = pl.BlockSpec((fan, width), lambda p, lens: (p, 0))
    return pl.pallas_call(
        kernel,
        out_shape=(out, out, out),
        grid_spec=pltpu.PrefetchScalarGridSpec(
            num_scalar_prefetch=1,
            grid=(count,),
            in_specs=[
                pl.BlockSpec((fan, width), lambda p, lens: (p + first, 0)),
                pl.BlockSpec((1, 1, cache_len, kv_width), lambda p, lens: (p + first, 0, 0, 0)),
                pl.BlockSpec((1, 1, cache_len, kv_width), lambda p, lens: (p + first, 1, 0, 0)),
            ],
            out_specs=[spec_out, spec_out, spec_out],
        ),
        cost_estimate=pl.CostEstimate(
            flops=4 * count * fan * width * cache_len,
            transcendentals=count * fan * width * cache_len // HEAD_SIZE,
            bytes_accessed=count * (2 * cache_len * kv_width * 2 + fan * width * 14),
        ),
    )(prompt_cache_length, queries, key_value_cache, key_value_cache)


def _swap(x, mask, count):
    return lax.ppermute(x, "tensor", perm=[(i, i ^ mask) for i in range(count)])


def per_device(
    partials,
    residual,
    attention_norm_gain,
    key_value_weight,
    adapter_down_weight,
    adapter_up_weight,
    row_adapter_index,
    queries,
    key_value_cache,
    prompt_cache_length,
):
    row_dev = residual.shape[0]
    model_width = residual.shape[1]
    tensor_count = lax.axis_size("tensor")
    quarter = model_width // tensor_count
    tensor_index = lax.axis_index("tensor")
    core = tensor_index % 2
    chip_x = tensor_index // 2
    local_heads = key_value_weight.shape[1]
    head_weight = jnp.transpose(key_value_weight, (1, 0, 2))

    half_rows = row_dev // 2
    part2 = partials[0].reshape(2, half_rows, model_width)
    mine_p = lax.dynamic_index_in_dim(part2, core, axis=0, keepdims=False)
    other_p = lax.dynamic_index_in_dim(part2, 1 - core, axis=0, keepdims=False)
    got_p = _swap(other_p, 1, tensor_count)
    chip_sum = mine_p.astype(jnp.float32) + got_p.astype(jnp.float32)
    far_sum = _swap(chip_sum.astype(jnp.bfloat16), 2, tensor_count)
    local_prompts = key_value_cache.shape[0]
    early_prompts = local_prompts // 2
    attention_early = cache_attention(
        queries, key_value_cache, prompt_cache_length, local_heads, FAN, 0, early_prompts
    )
    far_sum, head_weight, attention_early = lax.optimization_barrier(
        (far_sum, head_weight, attention_early)
    )
    res_half = lax.dynamic_index_in_dim(
        residual.reshape(2, half_rows, model_width), core, axis=0, keepdims=False
    )
    hidden_half = (
        res_half.astype(jnp.float32) + (chip_sum + far_sum.astype(jnp.float32))
    ).astype(jnp.bfloat16)
    hidden_wide = hidden_half.astype(jnp.float32)
    mean_sq = jnp.mean(hidden_wide * hidden_wide, axis=1, keepdims=True)
    normed_half = (
        hidden_wide * lax.rsqrt(mean_sq + EPSILON) * attention_norm_gain.astype(jnp.float32)
    ).astype(jnp.bfloat16)
    partner_quarter = lax.dynamic_slice_in_dim(
        hidden_half, (tensor_index ^ 1) * quarter, quarter, 1
    )
    swap_in = _swap(jnp.concatenate([normed_half, partner_quarter], axis=1), 1, tensor_count)
    normed_other = swap_in[:, :model_width]
    hidden_other = swap_in[:, model_width:]
    hidden_mine = lax.dynamic_slice_in_dim(hidden_half, tensor_index * quarter, quarter, 1)
    first = core == 0
    hidden_part = jnp.where(
        first,
        jnp.concatenate([hidden_mine, hidden_other], axis=0),
        jnp.concatenate([hidden_other, hidden_mine], axis=0),
    )
    normed_full = jnp.where(
        first,
        jnp.concatenate([normed_half, normed_other], axis=0),
        jnp.concatenate([normed_other, normed_half], axis=0),
    )
    normed_part = lax.dynamic_slice_in_dim(normed_full, tensor_index * quarter, quarter, 1)
    base_kv = jnp.einsum(
        "rf,hfd->rhd", normed_full, head_weight, preferred_element_type=jnp.float32
    ).reshape(row_dev, -1)

    adapt_count = lax.axis_size("adapter")
    capacity = max(2, 4 * row_dev // adapt_count)
    slot_count = adapt_count * capacity
    adapter_grouped = adapter_down_weight.shape[1] // ADAPTER_RANK
    owner_index = row_adapter_index // adapter_grouped
    local_id = row_adapter_index % adapter_grouped
    row_order = jnp.arange(row_dev)
    same_owner = owner_index[:, None] == owner_index[None, :]
    earlier = row_order[None, :] < row_order[:, None]
    slot_rank = jnp.sum((same_owner & earlier).astype(jnp.int32), axis=1)
    row_slot = owner_index * capacity + slot_rank
    row_to_slot = jnp.arange(slot_count)[:, None] == row_slot[None, :]
    slot_matrix = row_to_slot.astype(jnp.bfloat16)
    send_rows = jnp.dot(slot_matrix, normed_part, preferred_element_type=jnp.float32).astype(
        jnp.bfloat16
    )
    send_ids = jnp.sum(jnp.where(row_to_slot, local_id[None, :] + 1, 0), axis=1) - 1
    id_block = jnp.broadcast_to(send_ids.astype(jnp.bfloat16)[:, None], (slot_count, ID_LANES))
    payload = jnp.concatenate([send_rows, id_block], axis=1).reshape(
        adapt_count, capacity, quarter + ID_LANES
    )
    flattened_up = adapter_up_weight.reshape(adapter_grouped * ADAPTER_RANK, -1)
    rows_in = lax.all_to_all(payload, "adapter", split_axis=0, concat_axis=0, tiled=True)
    item_count = rows_in.shape[1]
    rows_in = rows_in.reshape(slot_count, quarter + ID_LANES)
    flattened_rows = rows_in[:, :quarter]
    ids_in = rows_in[:, quarter].astype(jnp.int32)
    adapter_pick = ids_in[:, None] == jnp.arange(adapter_grouped)[None, :]
    projected_rows = jnp.dot(
        flattened_rows, adapter_down_weight, preferred_element_type=jnp.float32
    ).reshape(-1, adapter_grouped, ADAPTER_RANK)
    partial_low = jnp.sum(jnp.where(adapter_pick[:, :, None], projected_rows, 0.0), axis=1)
    pair_low = partial_low + _swap(partial_low, 1, tensor_count)
    far_low, base_kv = lax.optimization_barrier((_swap(pair_low, 2, tensor_count), base_kv))
    reduced_rank_rows = (pair_low + far_low).astype(jnp.bfloat16)
    expanded_rows = jnp.where(
        adapter_pick[:, :, None], reduced_rank_rows[:, None, :], jnp.zeros((), jnp.bfloat16)
    ).reshape(-1, adapter_grouped * ADAPTER_RANK)
    adapter_update = (
        ADAPTER_SCALE * jnp.dot(expanded_rows, flattened_up, preferred_element_type=jnp.float32)
    ).astype(jnp.bfloat16)
    adapter_update = adapter_update.reshape(adapt_count, item_count, -1)
    returned = lax.all_to_all(adapter_update, "adapter", split_axis=0, concat_axis=0, tiled=True)
    attention_late = cache_attention(
        queries,
        key_value_cache,
        prompt_cache_length,
        local_heads,
        FAN,
        early_prompts,
        local_prompts - early_prompts,
    )
    returned, attention_late = lax.optimization_barrier((returned, attention_late))
    returned = returned.reshape(slot_count, -1)
    update_rows = lax.dot_general(
        slot_matrix, returned, (((0,), (0,)), ((), ())), preferred_element_type=jnp.float32
    )
    new_kv = (
        (base_kv + update_rows).astype(jnp.bfloat16).reshape(row_dev, local_heads, 2 * HEAD_SIZE)
    )

    group_size = queries.shape[1] // (local_heads * HEAD_SIZE)
    score_scale = HEAD_SIZE ** (-0.5)
    num_c, top_c, tot_c = [
        jnp.concatenate([early, late], axis=0)
        for early, late in zip(attention_early, attention_late)
    ]
    view = (row_dev, local_heads, group_size, HEAD_SIZE)
    cache_weighted = num_c.reshape(view)
    cache_top = top_c.reshape(view)[..., 0]
    cache_total = tot_c.reshape(view)[..., 0]
    query_heads = queries.reshape(view)
    own_key = new_kv[:, :, :HEAD_SIZE]
    own_value = new_kv[:, :, HEAD_SIZE:]
    own_score = (
        jnp.einsum("rkgd,rkd->rkg", query_heads, own_key, preferred_element_type=jnp.float32)
        * score_scale
    )
    score_top = jnp.maximum(cache_top, own_score)
    rescale = jnp.exp(cache_top - score_top)
    own_weight = jnp.exp(own_score - score_top).astype(jnp.bfloat16).astype(jnp.float32)
    weight_total = rescale * cache_total + own_weight
    weighted = (
        rescale[..., None] * cache_weighted
        + own_weight[..., None] * own_value.astype(jnp.float32)[:, :, None, :]
    )
    attended = (weighted / weight_total[..., None]).astype(jnp.bfloat16).reshape(row_dev, -1)
    return (hidden_part, new_kv, attended)


def solution(mesh):
    return jax.shard_map(
        per_device,
        mesh=mesh,
        in_specs=(
            P("tensor", "adapter", None),
            P("adapter", None),
            P(),
            P(None, "tensor", None),
            P("tensor", "adapter"),
            P("adapter", "tensor", None),
            P("adapter"),
            P("adapter", "tensor"),
            P("adapter", None, None, "tensor"),
            P("adapter"),
        ),
        out_specs=(P("adapter", "tensor"), P("adapter", "tensor", None), P("adapter", "tensor")),
        check_vma=False,
    )
```

```python
import functools

import jax
import jax.numpy as jnp
from jax import lax
from jax.experimental import pallas as pl
from jax.experimental.pallas import tpu as pltpu
from jax.sharding import PartitionSpec as P

HEAD_SIZE = 128
ADAPTER_RANK = 64
FAN = 8


EPSILON = 1e-05
ADAPTER_SCALE = 0.5
ID_LANES = 128


def _attn_kernel(len_ref, q_ref, k_ref, v_ref, num_ref, top_ref, tot_ref, *, heads, group, scale, first):
    p = pl.program_id(0) + first
    length = len_ref[p]
    fan = q_ref.shape[0]
    head_width = group * HEAD_SIZE
    for k in range(heads):
        lanes = pl.ds(k * HEAD_SIZE, HEAD_SIZE)
        qs = jnp.concatenate(
            [q_ref[:, pl.ds(k * head_width + g * HEAD_SIZE, HEAD_SIZE)] for g in range(group)], axis=0)
        kb = k_ref[0, 0, :, lanes]
        s = lax.dot_general(qs, kb, (((1,), (1,)), ((), ())), preferred_element_type=jnp.float32) * scale
        col = lax.broadcasted_iota(jnp.int32, s.shape, 1)
        s = jnp.where(col < length, s, -jnp.inf)
        m = jnp.max(s, axis=1, keepdims=True)
        w = jnp.exp(s - m).astype(jnp.bfloat16)
        tot = jnp.sum(w.astype(jnp.float32), axis=1, keepdims=True)
        num = jnp.dot(w, v_ref[0, 0, :, lanes], preferred_element_type=jnp.float32)
        for g in range(group):
            out_lanes = pl.ds(k * head_width + g * HEAD_SIZE, HEAD_SIZE)
            rows = slice(g * fan, (g + 1) * fan)
            num_ref[:, out_lanes] = num[rows]
            top_ref[:, out_lanes] = jnp.broadcast_to(m[rows], (fan, HEAD_SIZE))
            tot_ref[:, out_lanes] = jnp.broadcast_to(tot[rows], (fan, HEAD_SIZE))


def cache_attention(queries, key_value_cache, prompt_cache_length, local_heads, fan, first, count):
    _, _, cache_len, kv_width = key_value_cache.shape
    width = queries.shape[1]
    group = width // (local_heads * HEAD_SIZE)
    kernel = functools.partial(
        _attn_kernel, heads=local_heads, group=group, scale=HEAD_SIZE ** (-0.5), first=first)
    out = jax.ShapeDtypeStruct((count * fan, width), jnp.float32)
    spec_out = pl.BlockSpec((fan, width), lambda p, lens: (p, 0))
    return pl.pallas_call(
        kernel,
        out_shape=(out, out, out),
        grid_spec=pltpu.PrefetchScalarGridSpec(
            num_scalar_prefetch=1,
            grid=(count,),
            in_specs=[
                pl.BlockSpec((fan, width), lambda p, lens: (p + first, 0)),
                pl.BlockSpec((1, 1, cache_len, kv_width), lambda p, lens: (p + first, 0, 0, 0)),
                pl.BlockSpec((1, 1, cache_len, kv_width), lambda p, lens: (p + first, 1, 0, 0)),
            ],
            out_specs=[spec_out, spec_out, spec_out],
        ),
        cost_estimate=pl.CostEstimate(
            flops=4 * count * fan * width * cache_len,
            transcendentals=count * fan * width * cache_len // HEAD_SIZE,
            bytes_accessed=count * (2 * cache_len * kv_width * 2 + fan * width * 14),
        ),
    )(prompt_cache_length, queries, key_value_cache, key_value_cache)


def _swap(x, mask, count):
    return lax.ppermute(x, "tensor", perm=[(i, i ^ mask) for i in range(count)])


def per_device(
    partials,
    residual,
    attention_norm_gain,
    key_value_weight,
    adapter_down_weight,
    adapter_up_weight,
    row_adapter_index,
    queries,
    key_value_cache,
    prompt_cache_length,
):
    row_dev = residual.shape[0]
    model_width = residual.shape[1]
    tensor_count = lax.axis_size("tensor")
    quarter = model_width // tensor_count
    tensor_index = lax.axis_index("tensor")
    core = tensor_index % 2
    chip_x = tensor_index // 2
    local_heads = key_value_weight.shape[1]
    head_weight = jnp.transpose(key_value_weight, (1, 0, 2))

    half_rows = row_dev // 2
    own_partial = partials[0]
    rows_lo = own_partial[:half_rows]
    rows_hi = own_partial[half_rows:]
    to_core1 = [(i, i ^ 1) for i in range(0, tensor_count, 2)]
    to_core0 = [(i, i ^ 1) for i in range(1, tensor_count, 2)]
    got_hi = lax.ppermute(rows_hi, "tensor", perm=to_core1)
    got_lo = lax.ppermute(rows_lo, "tensor", perm=to_core0)
    first = core == 0
    mine_p = jnp.where(first, rows_lo, rows_hi)
    chip_sum = mine_p.astype(jnp.float32) + (got_lo.astype(jnp.float32) + got_hi.astype(jnp.float32))
    far_sum = _swap(chip_sum.astype(jnp.bfloat16), 2, tensor_count)
    local_prompts = key_value_cache.shape[0]
    early_prompts = local_prompts // 2
    attention_early = cache_attention(
        queries, key_value_cache, prompt_cache_length, local_heads, FAN, 0, early_prompts
    )
    far_sum, head_weight, attention_early = lax.optimization_barrier(
        (far_sum, head_weight, attention_early)
    )
    res_half = lax.dynamic_index_in_dim(
        residual.reshape(2, half_rows, model_width), core, axis=0, keepdims=False
    )
    hidden_half = (
        res_half.astype(jnp.float32) + (chip_sum + far_sum.astype(jnp.float32))
    ).astype(jnp.bfloat16)
    hidden_wide = hidden_half.astype(jnp.float32)
    mean_sq = jnp.mean(hidden_wide * hidden_wide, axis=1, keepdims=True)
    normed_half = (
        hidden_wide * lax.rsqrt(mean_sq + EPSILON) * attention_norm_gain.astype(jnp.float32)
    ).astype(jnp.bfloat16)
    partner_quarter = lax.dynamic_slice_in_dim(
        hidden_half, (tensor_index ^ 1) * quarter, quarter, 1
    )
    swap_in = _swap(jnp.concatenate([normed_half, partner_quarter], axis=1), 1, tensor_count)
    normed_other = swap_in[:, :model_width]
    hidden_other = swap_in[:, model_width:]
    hidden_mine = lax.dynamic_slice_in_dim(hidden_half, tensor_index * quarter, quarter, 1)
    hidden_part = jnp.where(
        first,
        jnp.concatenate([hidden_mine, hidden_other], axis=0),
        jnp.concatenate([hidden_other, hidden_mine], axis=0),
    )
    normed_full = jnp.where(
        first,
        jnp.concatenate([normed_half, normed_other], axis=0),
        jnp.concatenate([normed_other, normed_half], axis=0),
    )
    normed_part = lax.dynamic_slice_in_dim(normed_full, tensor_index * quarter, quarter, 1)
    base_kv = jnp.einsum(
        "rf,hfd->rhd", normed_full, head_weight, preferred_element_type=jnp.float32
    ).reshape(row_dev, -1)

    adapt_count = lax.axis_size("adapter")
    capacity = max(2, 4 * row_dev // adapt_count)
    slot_count = adapt_count * capacity
    adapter_grouped = adapter_down_weight.shape[1] // ADAPTER_RANK
    owner_index = row_adapter_index // adapter_grouped
    local_id = row_adapter_index % adapter_grouped
    row_order = jnp.arange(row_dev)
    same_owner = owner_index[:, None] == owner_index[None, :]
    earlier = row_order[None, :] < row_order[:, None]
    slot_rank = jnp.sum((same_owner & earlier).astype(jnp.int32), axis=1)
    row_slot = owner_index * capacity + slot_rank
    row_to_slot = jnp.arange(slot_count)[:, None] == row_slot[None, :]
    slot_matrix = row_to_slot.astype(jnp.bfloat16)
    send_rows = jnp.dot(slot_matrix, normed_part, preferred_element_type=jnp.float32).astype(
        jnp.bfloat16
    )
    send_ids = jnp.sum(jnp.where(row_to_slot, local_id[None, :] + 1, 0), axis=1) - 1
    id_block = jnp.broadcast_to(send_ids.astype(jnp.bfloat16)[:, None], (slot_count, ID_LANES))
    payload = jnp.concatenate([send_rows, id_block], axis=1).reshape(
        adapt_count, capacity, quarter + ID_LANES
    )
    flattened_up = adapter_up_weight.reshape(adapter_grouped * ADAPTER_RANK, -1)
    rows_in = lax.all_to_all(payload, "adapter", split_axis=0, concat_axis=0, tiled=True)
    item_count = rows_in.shape[1]
    rows_in = rows_in.reshape(slot_count, quarter + ID_LANES)
    flattened_rows = rows_in[:, :quarter]
    ids_in = rows_in[:, quarter].astype(jnp.int32)
    adapter_pick = ids_in[:, None] == jnp.arange(adapter_grouped)[None, :]
    projected_rows = jnp.dot(
        flattened_rows, adapter_down_weight, preferred_element_type=jnp.float32
    ).reshape(-1, adapter_grouped, ADAPTER_RANK)
    partial_low = jnp.sum(jnp.where(adapter_pick[:, :, None], projected_rows, 0.0), axis=1)
    pair_low = partial_low + _swap(partial_low, 1, tensor_count)
    far_low, base_kv = lax.optimization_barrier((_swap(pair_low, 2, tensor_count), base_kv))
    reduced_rank_rows = (pair_low + far_low).astype(jnp.bfloat16)
    expanded_rows = jnp.where(
        adapter_pick[:, :, None], reduced_rank_rows[:, None, :], jnp.zeros((), jnp.bfloat16)
    ).reshape(-1, adapter_grouped * ADAPTER_RANK)
    adapter_update = (
        ADAPTER_SCALE * jnp.dot(expanded_rows, flattened_up, preferred_element_type=jnp.float32)
    ).astype(jnp.bfloat16)
    adapter_update = adapter_update.reshape(adapt_count, item_count, -1)
    returned = lax.all_to_all(adapter_update, "adapter", split_axis=0, concat_axis=0, tiled=True)
    attention_late = cache_attention(
        queries,
        key_value_cache,
        prompt_cache_length,
        local_heads,
        FAN,
        early_prompts,
        local_prompts - early_prompts,
    )
    returned, attention_late = lax.optimization_barrier((returned, attention_late))
    returned = returned.reshape(slot_count, -1)
    update_rows = lax.dot_general(
        slot_matrix, returned, (((0,), (0,)), ((), ())), preferred_element_type=jnp.float32
    )
    new_kv = (
        (base_kv + update_rows).astype(jnp.bfloat16).reshape(row_dev, local_heads, 2 * HEAD_SIZE)
    )

    group_size = queries.shape[1] // (local_heads * HEAD_SIZE)
    score_scale = HEAD_SIZE ** (-0.5)
    num_c, top_c, tot_c = [
        jnp.concatenate([early, late], axis=0)
        for early, late in zip(attention_early, attention_late)
    ]
    view = (row_dev, local_heads, group_size, HEAD_SIZE)
    flat = (row_dev, local_heads * group_size, HEAD_SIZE)
    query_wide = queries.reshape(view).astype(jnp.float32)
    own_key = new_kv[:, :, :HEAD_SIZE].astype(jnp.float32)[:, :, None, :]
    own_value = jnp.broadcast_to(
        new_kv[:, :, HEAD_SIZE:].astype(jnp.float32)[:, :, None, :], view
    ).reshape(flat)
    own_score = (jnp.sum(query_wide * own_key, axis=-1) * score_scale).reshape(
        row_dev, local_heads * group_size, 1
    )
    cache_weighted = num_c.reshape(flat)
    cache_top = top_c.reshape(flat)
    cache_total = tot_c.reshape(flat)
    score_top = jnp.maximum(cache_top, own_score)
    rescale = jnp.exp(cache_top - score_top)
    own_weight = jnp.exp(own_score - score_top).astype(jnp.bfloat16).astype(jnp.float32)
    weight_total = rescale * cache_total + own_weight
    weighted = rescale * cache_weighted + own_weight * own_value
    attended = (weighted / weight_total).astype(jnp.bfloat16).reshape(row_dev, -1)
    return (hidden_part, new_kv, attended)


def solution(mesh):
    return jax.shard_map(
        per_device,
        mesh=mesh,
        in_specs=(
            P("tensor", "adapter", None),
            P("adapter", None),
            P(),
            P(None, "tensor", None),
            P("tensor", "adapter"),
            P("adapter", "tensor", None),
            P("adapter"),
            P("adapter", "tensor"),
            P("adapter", None, None, "tensor"),
            P("adapter"),
        ),
        out_specs=(P("adapter", "tensor"), P("adapter", "tensor", None), P("adapter", "tensor")),
        check_vma=False,
    )
```

```python
import functools

import jax
import jax.numpy as jnp
from jax import lax
from jax.experimental import pallas as pl
from jax.experimental.pallas import tpu as pltpu
from jax.sharding import PartitionSpec as P

HEAD_SIZE = 128
ADAPTER_RANK = 64
FAN = 8


EPSILON = 1e-05
ADAPTER_SCALE = 0.5
ID_LANES = 128


def _attn_kernel(len_ref, q_ref, k_ref, v_ref, num_ref, top_ref, tot_ref, *, heads, group, scale, first):
    p = pl.program_id(0) + first
    length = len_ref[p]
    fan = q_ref.shape[0]
    head_width = group * HEAD_SIZE
    for k in range(heads):
        lanes = pl.ds(k * HEAD_SIZE, HEAD_SIZE)
        qs = jnp.concatenate(
            [q_ref[:, pl.ds(k * head_width + g * HEAD_SIZE, HEAD_SIZE)] for g in range(group)], axis=0)
        kb = k_ref[0, 0, :, lanes]
        s = lax.dot_general(qs, kb, (((1,), (1,)), ((), ())), preferred_element_type=jnp.float32) * scale
        col = lax.broadcasted_iota(jnp.int32, s.shape, 1)
        s = jnp.where(col < length, s, -jnp.inf)
        m = jnp.max(s, axis=1, keepdims=True)
        w = jnp.exp(s - m).astype(jnp.bfloat16)
        tot = jnp.sum(w.astype(jnp.float32), axis=1, keepdims=True)
        num = jnp.dot(w, v_ref[0, 0, :, lanes], preferred_element_type=jnp.float32)
        for g in range(group):
            out_lanes = pl.ds(k * head_width + g * HEAD_SIZE, HEAD_SIZE)
            rows = slice(g * fan, (g + 1) * fan)
            num_ref[:, out_lanes] = num[rows]
            top_ref[:, out_lanes] = jnp.broadcast_to(m[rows], (fan, HEAD_SIZE))
            tot_ref[:, out_lanes] = jnp.broadcast_to(tot[rows], (fan, HEAD_SIZE))


def cache_attention(queries, key_value_cache, prompt_cache_length, local_heads, fan, first, count):
    _, _, cache_len, kv_width = key_value_cache.shape
    width = queries.shape[1]
    group = width // (local_heads * HEAD_SIZE)
    kernel = functools.partial(
        _attn_kernel, heads=local_heads, group=group, scale=HEAD_SIZE ** (-0.5), first=first)
    out = jax.ShapeDtypeStruct((count * fan, width), jnp.float32)
    spec_out = pl.BlockSpec((fan, width), lambda p, lens: (p, 0))
    return pl.pallas_call(
        kernel,
        out_shape=(out, out, out),
        grid_spec=pltpu.PrefetchScalarGridSpec(
            num_scalar_prefetch=1,
            grid=(count,),
            in_specs=[
                pl.BlockSpec((fan, width), lambda p, lens: (p + first, 0)),
                pl.BlockSpec((1, 1, cache_len, kv_width), lambda p, lens: (p + first, 0, 0, 0)),
                pl.BlockSpec((1, 1, cache_len, kv_width), lambda p, lens: (p + first, 1, 0, 0)),
            ],
            out_specs=[spec_out, spec_out, spec_out],
        ),
        cost_estimate=pl.CostEstimate(
            flops=4 * count * fan * width * cache_len,
            transcendentals=count * fan * width * cache_len // HEAD_SIZE,
            bytes_accessed=count * (2 * cache_len * kv_width * 2 + fan * width * 14),
        ),
    )(prompt_cache_length, queries, key_value_cache, key_value_cache)


def _swap(x, mask, count):
    return lax.ppermute(x, "tensor", perm=[(i, i ^ mask) for i in range(count)])


def per_device(
    partials,
    residual,
    attention_norm_gain,
    key_value_weight,
    adapter_down_weight,
    adapter_up_weight,
    row_adapter_index,
    queries,
    key_value_cache,
    prompt_cache_length,
):
    row_dev = residual.shape[0]
    model_width = residual.shape[1]
    tensor_count = lax.axis_size("tensor")
    quarter = model_width // tensor_count
    tensor_index = lax.axis_index("tensor")
    core = tensor_index % 2
    chip_x = tensor_index // 2
    local_heads = key_value_weight.shape[1]
    head_weight = jnp.transpose(key_value_weight, (1, 0, 2))

    half_rows = row_dev // 2
    part2 = partials[0].reshape(2, half_rows, model_width)
    mine_p = lax.dynamic_index_in_dim(part2, core, axis=0, keepdims=False)
    other_p = lax.dynamic_index_in_dim(part2, 1 - core, axis=0, keepdims=False)
    got_p = _swap(other_p, 1, tensor_count)
    chip_sum = mine_p.astype(jnp.float32) + got_p.astype(jnp.float32)
    far_sum = _swap(chip_sum.astype(jnp.bfloat16), 2, tensor_count)
    local_prompts = key_value_cache.shape[0]
    early_prompts = local_prompts // 2
    attention_early = cache_attention(
        queries, key_value_cache, prompt_cache_length, local_heads, FAN, 0, early_prompts
    )
    far_sum, head_weight, attention_early = lax.optimization_barrier(
        (far_sum, head_weight, attention_early)
    )
    res_half = lax.dynamic_index_in_dim(
        residual.reshape(2, half_rows, model_width), core, axis=0, keepdims=False
    )
    hidden_half = (
        res_half.astype(jnp.float32) + (chip_sum + far_sum.astype(jnp.float32))
    ).astype(jnp.bfloat16)
    hidden_wide = hidden_half.astype(jnp.float32)
    mean_sq = jnp.mean(hidden_wide * hidden_wide, axis=1, keepdims=True)
    normed_half = (
        hidden_wide * lax.rsqrt(mean_sq + EPSILON) * attention_norm_gain.astype(jnp.float32)
    ).astype(jnp.bfloat16)
    partner_quarter = lax.dynamic_slice_in_dim(
        hidden_half, (tensor_index ^ 1) * quarter, quarter, 1
    )
    swap_in = _swap(jnp.concatenate([normed_half, partner_quarter], axis=1), 1, tensor_count)
    normed_other = swap_in[:, :model_width]
    hidden_other = swap_in[:, model_width:]
    hidden_mine = lax.dynamic_slice_in_dim(hidden_half, tensor_index * quarter, quarter, 1)
    first = core == 0
    hidden_part = jnp.where(
        first,
        jnp.concatenate([hidden_mine, hidden_other], axis=0),
        jnp.concatenate([hidden_other, hidden_mine], axis=0),
    )
    normed_full = jnp.where(
        first,
        jnp.concatenate([normed_half, normed_other], axis=0),
        jnp.concatenate([normed_other, normed_half], axis=0),
    )
    normed_part = lax.dynamic_slice_in_dim(normed_full, tensor_index * quarter, quarter, 1)
    base_kv = jnp.einsum(
        "rf,hfd->rhd", normed_full, head_weight, preferred_element_type=jnp.float32
    ).reshape(row_dev, -1)

    adapt_count = lax.axis_size("adapter")
    capacity = max(2, 4 * row_dev // adapt_count)
    slot_count = adapt_count * capacity
    adapter_grouped = adapter_down_weight.shape[1] // ADAPTER_RANK
    owner_index = row_adapter_index // adapter_grouped
    local_id = row_adapter_index % adapter_grouped
    row_order = jnp.arange(row_dev)
    same_owner = owner_index[:, None] == owner_index[None, :]
    earlier = row_order[None, :] < row_order[:, None]
    slot_rank = jnp.sum((same_owner & earlier).astype(jnp.int32), axis=1)
    row_slot = owner_index * capacity + slot_rank
    row_to_slot = jnp.arange(slot_count)[:, None] == row_slot[None, :]
    slot_matrix = row_to_slot.astype(jnp.bfloat16)
    send_rows = jnp.dot(slot_matrix, normed_part, preferred_element_type=jnp.float32).astype(
        jnp.bfloat16
    )
    send_ids = jnp.sum(jnp.where(row_to_slot, local_id[None, :] + 1, 0), axis=1) - 1
    id_block = jnp.broadcast_to(send_ids.astype(jnp.bfloat16)[:, None], (slot_count, ID_LANES))
    payload = jnp.concatenate([send_rows, id_block], axis=1).reshape(
        adapt_count, capacity, quarter + ID_LANES
    )
    flattened_up = adapter_up_weight.reshape(adapter_grouped * ADAPTER_RANK, -1)
    rows_in = lax.all_to_all(payload, "adapter", split_axis=0, concat_axis=0, tiled=True)
    item_count = rows_in.shape[1]
    rows_in = rows_in.reshape(slot_count, quarter + ID_LANES)
    flattened_rows = rows_in[:, :quarter]
    ids_in = rows_in[:, quarter].astype(jnp.int32)
    adapter_pick = ids_in[:, None] == jnp.arange(adapter_grouped)[None, :]
    projected_rows = jnp.dot(
        flattened_rows, adapter_down_weight, preferred_element_type=jnp.float32
    ).reshape(-1, adapter_grouped, ADAPTER_RANK)
    partial_low = jnp.sum(jnp.where(adapter_pick[:, :, None], projected_rows, 0.0), axis=1)
    pair_low = partial_low + _swap(partial_low, 1, tensor_count)
    far_low, base_kv = lax.optimization_barrier((_swap(pair_low, 2, tensor_count), base_kv))
    reduced_rank_rows = (pair_low + far_low).astype(jnp.bfloat16)
    expanded_rows = jnp.where(
        adapter_pick[:, :, None], reduced_rank_rows[:, None, :], jnp.zeros((), jnp.bfloat16)
    ).reshape(-1, adapter_grouped * ADAPTER_RANK)
    adapter_update = (
        ADAPTER_SCALE * jnp.dot(expanded_rows, flattened_up, preferred_element_type=jnp.float32)
    ).astype(jnp.bfloat16)
    adapter_update = adapter_update.reshape(adapt_count, item_count, -1)
    returned = lax.all_to_all(adapter_update, "adapter", split_axis=0, concat_axis=0, tiled=True)
    adapter_update, queries_late = lax.optimization_barrier((adapter_update, queries))
    attention_late = cache_attention(
        queries_late,
        key_value_cache,
        prompt_cache_length,
        local_heads,
        FAN,
        early_prompts,
        local_prompts - early_prompts,
    )
    returned, attention_late = lax.optimization_barrier((returned, attention_late))
    returned = returned.reshape(slot_count, -1)
    update_rows = lax.dot_general(
        slot_matrix, returned, (((0,), (0,)), ((), ())), preferred_element_type=jnp.float32
    )
    new_kv = (
        (base_kv + update_rows).astype(jnp.bfloat16).reshape(row_dev, local_heads, 2 * HEAD_SIZE)
    )

    group_size = queries.shape[1] // (local_heads * HEAD_SIZE)
    score_scale = HEAD_SIZE ** (-0.5)
    num_c, top_c, tot_c = [
        jnp.concatenate([early, late], axis=0)
        for early, late in zip(attention_early, attention_late)
    ]
    view = (row_dev, local_heads, group_size, HEAD_SIZE)
    flat = (row_dev, local_heads * group_size, HEAD_SIZE)
    query_wide = queries.reshape(view).astype(jnp.float32)
    own_key = new_kv[:, :, :HEAD_SIZE].astype(jnp.float32)[:, :, None, :]
    own_value = jnp.broadcast_to(
        new_kv[:, :, HEAD_SIZE:].astype(jnp.float32)[:, :, None, :], view
    ).reshape(flat)
    own_score = (jnp.sum(query_wide * own_key, axis=-1) * score_scale).reshape(
        row_dev, local_heads * group_size, 1
    )
    cache_weighted = num_c.reshape(flat)
    cache_top = top_c.reshape(flat)
    cache_total = tot_c.reshape(flat)
    score_top = jnp.maximum(cache_top, own_score)
    rescale = jnp.exp(cache_top - score_top)
    own_weight = jnp.exp(own_score - score_top).astype(jnp.bfloat16).astype(jnp.float32)
    weight_total = rescale * cache_total + own_weight
    weighted = rescale * cache_weighted + own_weight * own_value
    attended = (weighted / weight_total).astype(jnp.bfloat16).reshape(row_dev, -1)
    return (hidden_part, new_kv, attended)


def solution(mesh):
    return jax.shard_map(
        per_device,
        mesh=mesh,
        in_specs=(
            P("tensor", "adapter", None),
            P("adapter", None),
            P(),
            P(None, "tensor", None),
            P("tensor", "adapter"),
            P("adapter", "tensor", None),
            P("adapter"),
            P("adapter", "tensor"),
            P("adapter", None, None, "tensor"),
            P("adapter"),
        ),
        out_specs=(P("adapter", "tensor"), P("adapter", "tensor", None), P("adapter", "tensor")),
        check_vma=False,
    )
```

```python
import functools

import jax
import jax.numpy as jnp
from jax import lax
from jax.experimental import pallas as pl
from jax.experimental.pallas import tpu as pltpu
from jax.sharding import PartitionSpec as P

HEAD_SIZE = 128
ADAPTER_RANK = 64
FAN = 8


EPSILON = 1e-05
ADAPTER_SCALE = 0.5
ID_LANES = 128


def _attn_kernel(len_ref, q_ref, k_ref, v_ref, num_ref, top_ref, tot_ref, *, heads, group, scale, first):
    p = pl.program_id(0) + first
    length = len_ref[p]
    fan = q_ref.shape[0]
    head_width = group * HEAD_SIZE
    for k in range(heads):
        lanes = pl.ds(k * HEAD_SIZE, HEAD_SIZE)
        qs = jnp.concatenate(
            [q_ref[:, pl.ds(k * head_width + g * HEAD_SIZE, HEAD_SIZE)] for g in range(group)], axis=0)
        kb = k_ref[0, 0, :, lanes]
        s = lax.dot_general(qs, kb, (((1,), (1,)), ((), ())), preferred_element_type=jnp.float32) * scale
        col = lax.broadcasted_iota(jnp.int32, s.shape, 1)
        s = jnp.where(col < length, s, -jnp.inf)
        m = jnp.max(s, axis=1, keepdims=True)
        w = jnp.exp(s - m).astype(jnp.bfloat16)
        tot = jnp.sum(w.astype(jnp.float32), axis=1, keepdims=True)
        num = jnp.dot(w, v_ref[0, 0, :, lanes], preferred_element_type=jnp.float32)
        for g in range(group):
            out_lanes = pl.ds(k * head_width + g * HEAD_SIZE, HEAD_SIZE)
            rows = slice(g * fan, (g + 1) * fan)
            num_ref[:, out_lanes] = num[rows]
            top_ref[:, out_lanes] = jnp.broadcast_to(m[rows], (fan, HEAD_SIZE))
            tot_ref[:, out_lanes] = jnp.broadcast_to(tot[rows], (fan, HEAD_SIZE))


def cache_attention(queries, key_value_cache, prompt_cache_length, local_heads, fan, first, count):
    _, _, cache_len, kv_width = key_value_cache.shape
    width = queries.shape[1]
    group = width // (local_heads * HEAD_SIZE)
    kernel = functools.partial(
        _attn_kernel, heads=local_heads, group=group, scale=HEAD_SIZE ** (-0.5), first=first)
    out = jax.ShapeDtypeStruct((count * fan, width), jnp.float32)
    spec_out = pl.BlockSpec((fan, width), lambda p, lens: (p, 0))
    return pl.pallas_call(
        kernel,
        out_shape=(out, out, out),
        grid_spec=pltpu.PrefetchScalarGridSpec(
            num_scalar_prefetch=1,
            grid=(count,),
            in_specs=[
                pl.BlockSpec((fan, width), lambda p, lens: (p + first, 0)),
                pl.BlockSpec((1, 1, cache_len, kv_width), lambda p, lens: (p + first, 0, 0, 0)),
                pl.BlockSpec((1, 1, cache_len, kv_width), lambda p, lens: (p + first, 1, 0, 0)),
            ],
            out_specs=[spec_out, spec_out, spec_out],
        ),
        cost_estimate=pl.CostEstimate(
            flops=4 * count * fan * width * cache_len,
            transcendentals=count * fan * width * cache_len // HEAD_SIZE,
            bytes_accessed=count * (2 * cache_len * kv_width * 2 + fan * width * 14),
        ),
    )(prompt_cache_length, queries, key_value_cache, key_value_cache)


def _swap(x, mask, count):
    return lax.ppermute(x, "tensor", perm=[(i, i ^ mask) for i in range(count)])


def per_device(
    partials,
    residual,
    attention_norm_gain,
    key_value_weight,
    adapter_down_weight,
    adapter_up_weight,
    row_adapter_index,
    queries,
    key_value_cache,
    prompt_cache_length,
):
    row_dev = residual.shape[0]
    model_width = residual.shape[1]
    tensor_count = lax.axis_size("tensor")
    quarter = model_width // tensor_count
    tensor_index = lax.axis_index("tensor")
    core = tensor_index % 2
    chip_x = tensor_index // 2
    local_heads = key_value_weight.shape[1]
    head_weight = jnp.transpose(key_value_weight, (1, 0, 2))

    half_rows = row_dev // 2
    part2 = partials[0].reshape(2, half_rows, model_width)
    mine_p = lax.dynamic_index_in_dim(part2, core, axis=0, keepdims=False)
    other_p = lax.dynamic_index_in_dim(part2, 1 - core, axis=0, keepdims=False)
    got_p = _swap(other_p, 1, tensor_count)
    chip_sum = mine_p.astype(jnp.float32) + got_p.astype(jnp.float32)
    far_sum = _swap(chip_sum.astype(jnp.bfloat16), 2, tensor_count)
    local_prompts = key_value_cache.shape[0]
    early_prompts = local_prompts // 2
    attention_early = cache_attention(
        queries, key_value_cache, prompt_cache_length, local_heads, FAN, 0, early_prompts
    )
    far_sum, head_weight, attention_early = lax.optimization_barrier(
        (far_sum, head_weight, attention_early)
    )
    res_half = lax.dynamic_index_in_dim(
        residual.reshape(2, half_rows, model_width), core, axis=0, keepdims=False
    )
    hidden_half = (
        res_half.astype(jnp.float32) + (chip_sum + far_sum.astype(jnp.float32))
    ).astype(jnp.bfloat16)
    hidden_wide = hidden_half.astype(jnp.float32)
    mean_sq = jnp.mean(hidden_wide * hidden_wide, axis=1, keepdims=True)
    normed_half = (
        hidden_wide * lax.rsqrt(mean_sq + EPSILON) * attention_norm_gain.astype(jnp.float32)
    ).astype(jnp.bfloat16)
    partner_quarter = lax.dynamic_slice_in_dim(
        hidden_half, (tensor_index ^ 1) * quarter, quarter, 1
    )
    swap_in = _swap(jnp.concatenate([normed_half, partner_quarter], axis=1), 1, tensor_count)
    normed_other = swap_in[:, :model_width]
    hidden_other = swap_in[:, model_width:]
    hidden_mine = lax.dynamic_slice_in_dim(hidden_half, tensor_index * quarter, quarter, 1)
    first = core == 0
    hidden_part = jnp.where(
        first,
        jnp.concatenate([hidden_mine, hidden_other], axis=0),
        jnp.concatenate([hidden_other, hidden_mine], axis=0),
    )
    normed_full = jnp.where(
        first,
        jnp.concatenate([normed_half, normed_other], axis=0),
        jnp.concatenate([normed_other, normed_half], axis=0),
    )
    normed_part = lax.dynamic_slice_in_dim(normed_full, tensor_index * quarter, quarter, 1)
    base_kv = jnp.einsum(
        "rf,hfd->rhd", normed_full, head_weight, preferred_element_type=jnp.float32
    ).reshape(row_dev, -1)

    adapt_count = lax.axis_size("adapter")
    capacity = max(2, 4 * row_dev // adapt_count)
    slot_count = adapt_count * capacity
    adapter_grouped = adapter_down_weight.shape[1] // ADAPTER_RANK
    owner_index = row_adapter_index // adapter_grouped
    local_id = row_adapter_index % adapter_grouped
    row_order = jnp.arange(row_dev)
    same_owner = owner_index[:, None] == owner_index[None, :]
    earlier = row_order[None, :] < row_order[:, None]
    slot_rank = jnp.sum((same_owner & earlier).astype(jnp.int32), axis=1)
    row_slot = owner_index * capacity + slot_rank
    row_to_slot = jnp.arange(slot_count)[:, None] == row_slot[None, :]
    slot_matrix = row_to_slot.astype(jnp.bfloat16)
    send_rows = jnp.dot(slot_matrix, normed_part, preferred_element_type=jnp.float32).astype(
        jnp.bfloat16
    )
    send_ids = jnp.sum(jnp.where(row_to_slot, local_id[None, :] + 1, 0), axis=1) - 1
    id_block = jnp.broadcast_to(send_ids.astype(jnp.bfloat16)[:, None], (slot_count, ID_LANES))
    payload = jnp.concatenate([send_rows, id_block], axis=1).reshape(
        adapt_count, capacity, quarter + ID_LANES
    )
    flattened_up = adapter_up_weight.reshape(adapter_grouped * ADAPTER_RANK, -1)
    payload, queries_late = lax.optimization_barrier((payload, queries))
    rows_in = lax.all_to_all(payload, "adapter", split_axis=0, concat_axis=0, tiled=True)
    attention_late = cache_attention(
        queries_late,
        key_value_cache,
        prompt_cache_length,
        local_heads,
        FAN,
        early_prompts,
        local_prompts - early_prompts,
    )
    rows_in, base_kv, attention_late = lax.optimization_barrier(
        (rows_in, base_kv, attention_late)
    )
    item_count = rows_in.shape[1]
    rows_in = rows_in.reshape(slot_count, quarter + ID_LANES)
    flattened_rows = rows_in[:, :quarter]
    ids_in = rows_in[:, quarter].astype(jnp.int32)
    adapter_pick = ids_in[:, None] == jnp.arange(adapter_grouped)[None, :]
    projected_rows = jnp.dot(
        flattened_rows, adapter_down_weight, preferred_element_type=jnp.float32
    ).reshape(-1, adapter_grouped, ADAPTER_RANK)
    partial_low = jnp.sum(jnp.where(adapter_pick[:, :, None], projected_rows, 0.0), axis=1)
    pair_low = partial_low + _swap(partial_low, 1, tensor_count)
    reduced_rank_rows = (pair_low + _swap(pair_low, 2, tensor_count)).astype(jnp.bfloat16)
    expanded_rows = jnp.where(
        adapter_pick[:, :, None], reduced_rank_rows[:, None, :], jnp.zeros((), jnp.bfloat16)
    ).reshape(-1, adapter_grouped * ADAPTER_RANK)
    adapter_update = (
        ADAPTER_SCALE * jnp.dot(expanded_rows, flattened_up, preferred_element_type=jnp.float32)
    ).astype(jnp.bfloat16)
    adapter_update = adapter_update.reshape(adapt_count, item_count, -1)
    returned = lax.all_to_all(adapter_update, "adapter", split_axis=0, concat_axis=0, tiled=True)
    returned = returned.reshape(slot_count, -1)
    update_rows = lax.dot_general(
        slot_matrix, returned, (((0,), (0,)), ((), ())), preferred_element_type=jnp.float32
    )
    new_kv = (
        (base_kv + update_rows).astype(jnp.bfloat16).reshape(row_dev, local_heads, 2 * HEAD_SIZE)
    )

    group_size = queries.shape[1] // (local_heads * HEAD_SIZE)
    score_scale = HEAD_SIZE ** (-0.5)
    num_c, top_c, tot_c = [
        jnp.concatenate([early, late], axis=0)
        for early, late in zip(attention_early, attention_late)
    ]
    view = (row_dev, local_heads, group_size, HEAD_SIZE)
    flat = (row_dev, local_heads * group_size, HEAD_SIZE)
    query_wide = queries.reshape(view).astype(jnp.float32)
    own_key = new_kv[:, :, :HEAD_SIZE].astype(jnp.float32)[:, :, None, :]
    own_value = jnp.broadcast_to(
        new_kv[:, :, HEAD_SIZE:].astype(jnp.float32)[:, :, None, :], view
    ).reshape(flat)
    own_score = (jnp.sum(query_wide * own_key, axis=-1) * score_scale).reshape(
        row_dev, local_heads * group_size, 1
    )
    cache_weighted = num_c.reshape(flat)
    cache_top = top_c.reshape(flat)
    cache_total = tot_c.reshape(flat)
    score_top = jnp.maximum(cache_top, own_score)
    rescale = jnp.exp(cache_top - score_top)
    own_weight = jnp.exp(own_score - score_top).astype(jnp.bfloat16).astype(jnp.float32)
    weight_total = rescale * cache_total + own_weight
    weighted = rescale * cache_weighted + own_weight * own_value
    attended = (weighted / weight_total).astype(jnp.bfloat16).reshape(row_dev, -1)
    return (hidden_part, new_kv, attended)


def solution(mesh):
    return jax.shard_map(
        per_device,
        mesh=mesh,
        in_specs=(
            P("tensor", "adapter", None),
            P("adapter", None),
            P(),
            P(None, "tensor", None),
            P("tensor", "adapter"),
            P("adapter", "tensor", None),
            P("adapter"),
            P("adapter", "tensor"),
            P("adapter", None, None, "tensor"),
            P("adapter"),
        ),
        out_specs=(P("adapter", "tensor"), P("adapter", "tensor", None), P("adapter", "tensor")),
        check_vma=False,
    )
```

```python
import functools

import jax
import jax.numpy as jnp
from jax import lax
from jax.experimental import pallas as pl
from jax.experimental.pallas import tpu as pltpu
from jax.sharding import PartitionSpec as P

HEAD_SIZE = 128
ADAPTER_RANK = 64
FAN = 8


EPSILON = 1e-05
ADAPTER_SCALE = 0.5
ID_LANES = 128


def _attn_kernel(len_ref, q_ref, k_ref, v_ref, num_ref, top_ref, tot_ref, *, heads, group, scale, first):
    p = pl.program_id(0) + first
    length = len_ref[p]
    fan = q_ref.shape[0]
    head_width = group * HEAD_SIZE
    for k in range(heads):
        lanes = pl.ds(k * HEAD_SIZE, HEAD_SIZE)
        qs = jnp.concatenate(
            [q_ref[:, pl.ds(k * head_width + g * HEAD_SIZE, HEAD_SIZE)] for g in range(group)], axis=0)
        kb = k_ref[0, 0, :, lanes]
        s = lax.dot_general(qs, kb, (((1,), (1,)), ((), ())), preferred_element_type=jnp.float32) * scale
        col = lax.broadcasted_iota(jnp.int32, s.shape, 1)
        s = jnp.where(col < length, s, -jnp.inf)
        m = jnp.max(s, axis=1, keepdims=True)
        w = jnp.exp(s - m).astype(jnp.bfloat16)
        tot = jnp.sum(w.astype(jnp.float32), axis=1, keepdims=True)
        num = jnp.dot(w, v_ref[0, 0, :, lanes], preferred_element_type=jnp.float32)
        for g in range(group):
            out_lanes = pl.ds(k * head_width + g * HEAD_SIZE, HEAD_SIZE)
            rows = slice(g * fan, (g + 1) * fan)
            num_ref[:, out_lanes] = num[rows]
            top_ref[:, out_lanes] = jnp.broadcast_to(m[rows], (fan, HEAD_SIZE))
            tot_ref[:, out_lanes] = jnp.broadcast_to(tot[rows], (fan, HEAD_SIZE))


def cache_attention(queries, key_value_cache, prompt_cache_length, local_heads, fan, first, count):
    _, _, cache_len, kv_width = key_value_cache.shape
    width = queries.shape[1]
    group = width // (local_heads * HEAD_SIZE)
    kernel = functools.partial(
        _attn_kernel, heads=local_heads, group=group, scale=HEAD_SIZE ** (-0.5), first=first)
    out = jax.ShapeDtypeStruct((count * fan, width), jnp.float32)
    spec_out = pl.BlockSpec((fan, width), lambda p, lens: (p, 0))
    return pl.pallas_call(
        kernel,
        out_shape=(out, out, out),
        grid_spec=pltpu.PrefetchScalarGridSpec(
            num_scalar_prefetch=1,
            grid=(count,),
            in_specs=[
                pl.BlockSpec((fan, width), lambda p, lens: (p + first, 0)),
                pl.BlockSpec((1, 1, cache_len, kv_width), lambda p, lens: (p + first, 0, 0, 0)),
                pl.BlockSpec((1, 1, cache_len, kv_width), lambda p, lens: (p + first, 1, 0, 0)),
            ],
            out_specs=[spec_out, spec_out, spec_out],
        ),
        cost_estimate=pl.CostEstimate(
            flops=4 * count * fan * width * cache_len,
            transcendentals=count * fan * width * cache_len // HEAD_SIZE,
            bytes_accessed=count * (2 * cache_len * kv_width * 2 + fan * width * 14),
        ),
    )(prompt_cache_length, queries, key_value_cache, key_value_cache)


def _swap(x, mask, count):
    return lax.ppermute(x, "tensor", perm=[(i, i ^ mask) for i in range(count)])


def per_device(
    partials,
    residual,
    attention_norm_gain,
    key_value_weight,
    adapter_down_weight,
    adapter_up_weight,
    row_adapter_index,
    queries,
    key_value_cache,
    prompt_cache_length,
):
    row_dev = residual.shape[0]
    model_width = residual.shape[1]
    tensor_count = lax.axis_size("tensor")
    quarter = model_width // tensor_count
    tensor_index = lax.axis_index("tensor")
    core = tensor_index % 2
    chip_x = tensor_index // 2
    local_heads = key_value_weight.shape[1]
    head_weight = jnp.transpose(key_value_weight, (1, 0, 2))

    half_rows = row_dev // 2
    part2 = partials[0].reshape(2, half_rows, model_width)
    mine_p = lax.dynamic_index_in_dim(part2, core, axis=0, keepdims=False)
    other_p = lax.dynamic_index_in_dim(part2, 1 - core, axis=0, keepdims=False)
    got_p = _swap(other_p, 1, tensor_count)
    chip_sum = mine_p.astype(jnp.float32) + got_p.astype(jnp.float32)
    far_sum = _swap(chip_sum.astype(jnp.bfloat16), 2, tensor_count)
    local_prompts = key_value_cache.shape[0]
    early_prompts = local_prompts // 2
    attention_early = cache_attention(
        queries, key_value_cache, prompt_cache_length, local_heads, FAN, 0, early_prompts
    )
    far_sum, head_weight, attention_early = lax.optimization_barrier(
        (far_sum, head_weight, attention_early)
    )
    res_half = lax.dynamic_index_in_dim(
        residual.reshape(2, half_rows, model_width), core, axis=0, keepdims=False
    )
    hidden_half = (
        res_half.astype(jnp.float32) + (chip_sum + far_sum.astype(jnp.float32))
    ).astype(jnp.bfloat16)
    hidden_wide = hidden_half.astype(jnp.float32)
    mean_sq = jnp.mean(hidden_wide * hidden_wide, axis=1, keepdims=True)
    normed_half = (
        hidden_wide * lax.rsqrt(mean_sq + EPSILON) * attention_norm_gain.astype(jnp.float32)
    ).astype(jnp.bfloat16)
    partner_quarter = lax.dynamic_slice_in_dim(
        hidden_half, (tensor_index ^ 1) * quarter, quarter, 1
    )
    swap_in = _swap(jnp.concatenate([normed_half, partner_quarter], axis=1), 1, tensor_count)
    normed_other = swap_in[:, :model_width]
    hidden_other = swap_in[:, model_width:]
    hidden_mine = lax.dynamic_slice_in_dim(hidden_half, tensor_index * quarter, quarter, 1)
    first = core == 0
    hidden_part = jnp.where(
        first,
        jnp.concatenate([hidden_mine, hidden_other], axis=0),
        jnp.concatenate([hidden_other, hidden_mine], axis=0),
    )
    normed_full = jnp.where(
        first,
        jnp.concatenate([normed_half, normed_other], axis=0),
        jnp.concatenate([normed_other, normed_half], axis=0),
    )
    normed_part = lax.dynamic_slice_in_dim(normed_full, tensor_index * quarter, quarter, 1)
    base_kv = jnp.einsum(
        "rf,hfd->rhd", normed_full, head_weight, preferred_element_type=jnp.float32
    ).reshape(row_dev, -1)

    adapt_count = lax.axis_size("adapter")
    capacity = max(2, 4 * row_dev // adapt_count)
    slot_count = adapt_count * capacity
    adapter_grouped = adapter_down_weight.shape[1] // ADAPTER_RANK
    owner_index = row_adapter_index // adapter_grouped
    local_id = row_adapter_index % adapter_grouped
    row_order = jnp.arange(row_dev)
    same_owner = owner_index[:, None] == owner_index[None, :]
    earlier = row_order[None, :] < row_order[:, None]
    slot_rank = jnp.sum((same_owner & earlier).astype(jnp.int32), axis=1)
    row_slot = owner_index * capacity + slot_rank
    row_to_slot = jnp.arange(slot_count)[:, None] == row_slot[None, :]
    slot_matrix = row_to_slot.astype(jnp.bfloat16)
    send_rows = jnp.dot(slot_matrix, normed_part, preferred_element_type=jnp.float32).astype(
        jnp.bfloat16
    )
    send_ids = jnp.sum(jnp.where(row_to_slot, local_id[None, :] + 1, 0), axis=1) - 1
    id_block = jnp.broadcast_to(send_ids.astype(jnp.bfloat16)[:, None], (slot_count, ID_LANES))
    payload = jnp.concatenate([send_rows, id_block], axis=1).reshape(
        adapt_count, capacity, quarter + ID_LANES
    )
    flattened_up = adapter_up_weight.reshape(adapter_grouped * ADAPTER_RANK, -1)
    payload, queries_late = lax.optimization_barrier((payload, queries))
    rows_in = lax.all_to_all(payload, "adapter", split_axis=0, concat_axis=0, tiled=True)
    attention_late = cache_attention(
        queries_late,
        key_value_cache,
        prompt_cache_length,
        local_heads,
        FAN,
        early_prompts,
        local_prompts - early_prompts,
    )
    rows_in, base_kv, attention_late = lax.optimization_barrier(
        (rows_in, base_kv, attention_late)
    )
    item_count = rows_in.shape[1]
    rows_in = rows_in.reshape(slot_count, quarter + ID_LANES)
    flattened_rows = rows_in[:, :quarter]
    ids_in = rows_in[:, quarter].astype(jnp.int32)
    adapter_pick = ids_in[:, None] == jnp.arange(adapter_grouped)[None, :]
    projected_rows = jnp.dot(
        flattened_rows, adapter_down_weight, preferred_element_type=jnp.float32
    ).reshape(-1, adapter_grouped, ADAPTER_RANK)
    partial_low = jnp.sum(jnp.where(adapter_pick[:, :, None], projected_rows, 0.0), axis=1)
    low_core = _swap(partial_low, 1, tensor_count)
    low_chip = _swap(partial_low, 2, tensor_count)
    low_diag = _swap(partial_low, 3, tensor_count)
    reduced_rank_rows = ((partial_low + low_core) + (low_chip + low_diag)).astype(jnp.bfloat16)
    expanded_rows = jnp.where(
        adapter_pick[:, :, None], reduced_rank_rows[:, None, :], jnp.zeros((), jnp.bfloat16)
    ).reshape(-1, adapter_grouped * ADAPTER_RANK)
    adapter_update = (
        ADAPTER_SCALE * jnp.dot(expanded_rows, flattened_up, preferred_element_type=jnp.float32)
    ).astype(jnp.bfloat16)
    adapter_update = adapter_update.reshape(adapt_count, item_count, -1)
    returned = lax.all_to_all(adapter_update, "adapter", split_axis=0, concat_axis=0, tiled=True)
    returned = returned.reshape(slot_count, -1)
    update_rows = lax.dot_general(
        slot_matrix, returned, (((0,), (0,)), ((), ())), preferred_element_type=jnp.float32
    )
    new_kv = (
        (base_kv + update_rows).astype(jnp.bfloat16).reshape(row_dev, local_heads, 2 * HEAD_SIZE)
    )

    group_size = queries.shape[1] // (local_heads * HEAD_SIZE)
    score_scale = HEAD_SIZE ** (-0.5)
    num_c, top_c, tot_c = [
        jnp.concatenate([early, late], axis=0)
        for early, late in zip(attention_early, attention_late)
    ]
    view = (row_dev, local_heads, group_size, HEAD_SIZE)
    flat = (row_dev, local_heads * group_size, HEAD_SIZE)
    query_wide = queries.reshape(view).astype(jnp.float32)
    own_key = new_kv[:, :, :HEAD_SIZE].astype(jnp.float32)[:, :, None, :]
    own_value = jnp.broadcast_to(
        new_kv[:, :, HEAD_SIZE:].astype(jnp.float32)[:, :, None, :], view
    ).reshape(flat)
    own_score = (jnp.sum(query_wide * own_key, axis=-1) * score_scale).reshape(
        row_dev, local_heads * group_size, 1
    )
    cache_weighted = num_c.reshape(flat)
    cache_top = top_c.reshape(flat)
    cache_total = tot_c.reshape(flat)
    score_top = jnp.maximum(cache_top, own_score)
    rescale = jnp.exp(cache_top - score_top)
    own_weight = jnp.exp(own_score - score_top).astype(jnp.bfloat16).astype(jnp.float32)
    weight_total = rescale * cache_total + own_weight
    weighted = rescale * cache_weighted + own_weight * own_value
    attended = (weighted / weight_total).astype(jnp.bfloat16).reshape(row_dev, -1)
    return (hidden_part, new_kv, attended)


def solution(mesh):
    return jax.shard_map(
        per_device,
        mesh=mesh,
        in_specs=(
            P("tensor", "adapter", None),
            P("adapter", None),
            P(),
            P(None, "tensor", None),
            P("tensor", "adapter"),
            P("adapter", "tensor", None),
            P("adapter"),
            P("adapter", "tensor"),
            P("adapter", None, None, "tensor"),
            P("adapter"),
        ),
        out_specs=(P("adapter", "tensor"), P("adapter", "tensor", None), P("adapter", "tensor")),
        check_vma=False,
    )
```

```python
import functools

import jax
import jax.numpy as jnp
from jax import lax
from jax.experimental import pallas as pl
from jax.experimental.pallas import tpu as pltpu
from jax.sharding import PartitionSpec as P

HEAD_SIZE = 128
ADAPTER_RANK = 64
FAN = 8


EPSILON = 1e-05
ADAPTER_SCALE = 0.5
ID_LANES = 128


def _attn_kernel(len_ref, q_ref, k_ref, v_ref, num_ref, top_ref, tot_ref, *, heads, group, scale, first):
    p = pl.program_id(0) + first
    length = len_ref[p]
    fan = q_ref.shape[0]
    head_width = group * HEAD_SIZE
    for k in range(heads):
        lanes = pl.ds(k * HEAD_SIZE, HEAD_SIZE)
        qs = jnp.concatenate(
            [q_ref[:, pl.ds(k * head_width + g * HEAD_SIZE, HEAD_SIZE)] for g in range(group)], axis=0)
        kb = k_ref[0, 0, :, lanes]
        s = lax.dot_general(qs, kb, (((1,), (1,)), ((), ())), preferred_element_type=jnp.float32) * scale
        col = lax.broadcasted_iota(jnp.int32, s.shape, 1)
        s = jnp.where(col < length, s, -jnp.inf)
        m = jnp.max(s, axis=1, keepdims=True)
        w = jnp.exp(s - m).astype(jnp.bfloat16)
        tot = jnp.sum(w.astype(jnp.float32), axis=1, keepdims=True)
        num = jnp.dot(w, v_ref[0, 0, :, lanes], preferred_element_type=jnp.float32)
        for g in range(group):
            out_lanes = pl.ds(k * head_width + g * HEAD_SIZE, HEAD_SIZE)
            rows = slice(g * fan, (g + 1) * fan)
            num_ref[:, out_lanes] = num[rows]
            top_ref[:, out_lanes] = jnp.broadcast_to(m[rows], (fan, HEAD_SIZE))
            tot_ref[:, out_lanes] = jnp.broadcast_to(tot[rows], (fan, HEAD_SIZE))


def cache_attention(queries, key_value_cache, prompt_cache_length, local_heads, fan, first, count):
    _, _, cache_len, kv_width = key_value_cache.shape
    width = queries.shape[1]
    group = width // (local_heads * HEAD_SIZE)
    kernel = functools.partial(
        _attn_kernel, heads=local_heads, group=group, scale=HEAD_SIZE ** (-0.5), first=first)
    out = jax.ShapeDtypeStruct((count * fan, width), jnp.float32)
    spec_out = pl.BlockSpec((fan, width), lambda p, lens: (p, 0))
    return pl.pallas_call(
        kernel,
        out_shape=(out, out, out),
        grid_spec=pltpu.PrefetchScalarGridSpec(
            num_scalar_prefetch=1,
            grid=(count,),
            in_specs=[
                pl.BlockSpec((fan, width), lambda p, lens: (p + first, 0)),
                pl.BlockSpec((1, 1, cache_len, kv_width), lambda p, lens: (p + first, 0, 0, 0)),
                pl.BlockSpec((1, 1, cache_len, kv_width), lambda p, lens: (p + first, 1, 0, 0)),
            ],
            out_specs=[spec_out, spec_out, spec_out],
        ),
        cost_estimate=pl.CostEstimate(
            flops=4 * count * fan * width * cache_len,
            transcendentals=count * fan * width * cache_len // HEAD_SIZE,
            bytes_accessed=count * (2 * cache_len * kv_width * 2 + fan * width * 14),
        ),
    )(prompt_cache_length, queries, key_value_cache, key_value_cache)


def _down_kernel(rows_ref, weight_ref, out_ref, *, width, groups):
    ids = rows_ref[:, pl.ds(width, 1)].astype(jnp.float32).astype(jnp.int32)
    proj = jnp.dot(rows_ref[:, pl.ds(0, width)], weight_ref[...], preferred_element_type=jnp.float32)
    lane = lax.broadcasted_iota(jnp.int32, (proj.shape[0], 2 * ADAPTER_RANK), 1)
    upper = (lane >= ADAPTER_RANK).astype(jnp.int32)
    acc = jnp.zeros((proj.shape[0], 2 * ADAPTER_RANK), jnp.float32)
    for j in range(groups // 2):
        block = proj[:, j * 2 * ADAPTER_RANK:(j + 1) * 2 * ADAPTER_RANK]
        acc = acc + jnp.where(ids == 2 * j + upper, block, 0.0)
    out_ref[...] = acc


def down_project(rows_in, down_weight, width):
    slots = rows_in.shape[0]
    groups = down_weight.shape[1] // ADAPTER_RANK
    kernel = functools.partial(_down_kernel, width=width, groups=groups)
    folded = pl.pallas_call(
        kernel,
        out_shape=jax.ShapeDtypeStruct((slots, 2 * ADAPTER_RANK), jnp.float32),
        in_specs=[pl.BlockSpec(memory_space=pltpu.VMEM), pl.BlockSpec(memory_space=pltpu.VMEM)],
        out_specs=pl.BlockSpec(memory_space=pltpu.VMEM),
        cost_estimate=pl.CostEstimate(
            flops=2 * slots * width * down_weight.shape[1],
            transcendentals=0,
            bytes_accessed=rows_in.size * 2 + down_weight.size * 2 + slots * 512,
        ),
    )(rows_in, down_weight)
    return folded[:, :ADAPTER_RANK] + folded[:, ADAPTER_RANK:]


def _swap(x, mask, count):
    return lax.ppermute(x, "tensor", perm=[(i, i ^ mask) for i in range(count)])


def per_device(
    partials,
    residual,
    attention_norm_gain,
    key_value_weight,
    adapter_down_weight,
    adapter_up_weight,
    row_adapter_index,
    queries,
    key_value_cache,
    prompt_cache_length,
):
    row_dev = residual.shape[0]
    model_width = residual.shape[1]
    tensor_count = lax.axis_size("tensor")
    quarter = model_width // tensor_count
    tensor_index = lax.axis_index("tensor")
    core = tensor_index % 2
    chip_x = tensor_index // 2
    local_heads = key_value_weight.shape[1]
    head_weight = jnp.transpose(key_value_weight, (1, 0, 2))

    half_rows = row_dev // 2
    part2 = partials[0].reshape(2, half_rows, model_width)
    mine_p = lax.dynamic_index_in_dim(part2, core, axis=0, keepdims=False)
    other_p = lax.dynamic_index_in_dim(part2, 1 - core, axis=0, keepdims=False)
    got_p = _swap(other_p, 1, tensor_count)
    chip_sum = mine_p.astype(jnp.float32) + got_p.astype(jnp.float32)
    far_sum = _swap(chip_sum.astype(jnp.bfloat16), 2, tensor_count)
    local_prompts = key_value_cache.shape[0]
    early_prompts = local_prompts // 2
    attention_early = cache_attention(
        queries, key_value_cache, prompt_cache_length, local_heads, FAN, 0, early_prompts
    )
    far_sum, head_weight, attention_early = lax.optimization_barrier(
        (far_sum, head_weight, attention_early)
    )
    res_half = lax.dynamic_index_in_dim(
        residual.reshape(2, half_rows, model_width), core, axis=0, keepdims=False
    )
    hidden_half = (
        res_half.astype(jnp.float32) + (chip_sum + far_sum.astype(jnp.float32))
    ).astype(jnp.bfloat16)
    hidden_wide = hidden_half.astype(jnp.float32)
    mean_sq = jnp.mean(hidden_wide * hidden_wide, axis=1, keepdims=True)
    normed_half = (
        hidden_wide * lax.rsqrt(mean_sq + EPSILON) * attention_norm_gain.astype(jnp.float32)
    ).astype(jnp.bfloat16)
    partner_quarter = lax.dynamic_slice_in_dim(
        hidden_half, (tensor_index ^ 1) * quarter, quarter, 1
    )
    swap_in = _swap(jnp.concatenate([normed_half, partner_quarter], axis=1), 1, tensor_count)
    normed_other = swap_in[:, :model_width]
    hidden_other = swap_in[:, model_width:]
    hidden_mine = lax.dynamic_slice_in_dim(hidden_half, tensor_index * quarter, quarter, 1)
    first = core == 0
    hidden_part = jnp.where(
        first,
        jnp.concatenate([hidden_mine, hidden_other], axis=0),
        jnp.concatenate([hidden_other, hidden_mine], axis=0),
    )
    normed_full = jnp.where(
        first,
        jnp.concatenate([normed_half, normed_other], axis=0),
        jnp.concatenate([normed_other, normed_half], axis=0),
    )
    normed_part = lax.dynamic_slice_in_dim(normed_full, tensor_index * quarter, quarter, 1)
    base_kv = jnp.einsum(
        "rf,hfd->rhd", normed_full, head_weight, preferred_element_type=jnp.float32
    ).reshape(row_dev, -1)

    adapt_count = lax.axis_size("adapter")
    capacity = max(2, 4 * row_dev // adapt_count)
    slot_count = adapt_count * capacity
    adapter_grouped = adapter_down_weight.shape[1] // ADAPTER_RANK
    owner_index = row_adapter_index // adapter_grouped
    local_id = row_adapter_index % adapter_grouped
    row_order = jnp.arange(row_dev)
    same_owner = owner_index[:, None] == owner_index[None, :]
    earlier = row_order[None, :] < row_order[:, None]
    slot_rank = jnp.sum((same_owner & earlier).astype(jnp.int32), axis=1)
    row_slot = owner_index * capacity + slot_rank
    row_to_slot = jnp.arange(slot_count)[:, None] == row_slot[None, :]
    slot_matrix = row_to_slot.astype(jnp.bfloat16)
    send_rows = jnp.dot(slot_matrix, normed_part, preferred_element_type=jnp.float32).astype(
        jnp.bfloat16
    )
    send_ids = jnp.sum(jnp.where(row_to_slot, local_id[None, :] + 1, 0), axis=1) - 1
    id_block = jnp.broadcast_to(send_ids.astype(jnp.bfloat16)[:, None], (slot_count, ID_LANES))
    payload = jnp.concatenate([send_rows, id_block], axis=1).reshape(
        adapt_count, capacity, quarter + ID_LANES
    )
    flattened_up = adapter_up_weight.reshape(adapter_grouped * ADAPTER_RANK, -1)
    payload, queries_late = lax.optimization_barrier((payload, queries))
    rows_in = lax.all_to_all(payload, "adapter", split_axis=0, concat_axis=0, tiled=True)
    attention_late = cache_attention(
        queries_late,
        key_value_cache,
        prompt_cache_length,
        local_heads,
        FAN,
        early_prompts,
        local_prompts - early_prompts,
    )
    rows_in, base_kv, attention_late = lax.optimization_barrier(
        (rows_in, base_kv, attention_late)
    )
    item_count = rows_in.shape[1]
    rows_in = rows_in.reshape(slot_count, quarter + ID_LANES)
    ids_in = rows_in[:, quarter].astype(jnp.int32)
    adapter_pick = ids_in[:, None] == jnp.arange(adapter_grouped)[None, :]
    partial_low = down_project(rows_in, adapter_down_weight, quarter)
    low_core = _swap(partial_low, 1, tensor_count)
    low_chip = _swap(partial_low, 2, tensor_count)
    low_diag = _swap(partial_low, 3, tensor_count)
    reduced_rank_rows = ((partial_low + low_core) + (low_chip + low_diag)).astype(jnp.bfloat16)
    expanded_rows = jnp.where(
        adapter_pick[:, :, None], reduced_rank_rows[:, None, :], jnp.zeros((), jnp.bfloat16)
    ).reshape(-1, adapter_grouped * ADAPTER_RANK)
    adapter_update = (
        ADAPTER_SCALE * jnp.dot(expanded_rows, flattened_up, preferred_element_type=jnp.float32)
    ).astype(jnp.bfloat16)
    adapter_update = adapter_update.reshape(adapt_count, item_count, -1)
    returned = lax.all_to_all(adapter_update, "adapter", split_axis=0, concat_axis=0, tiled=True)
    returned = returned.reshape(slot_count, -1)
    update_rows = lax.dot_general(
        slot_matrix, returned, (((0,), (0,)), ((), ())), preferred_element_type=jnp.float32
    )
    new_kv = (
        (base_kv + update_rows).astype(jnp.bfloat16).reshape(row_dev, local_heads, 2 * HEAD_SIZE)
    )

    group_size = queries.shape[1] // (local_heads * HEAD_SIZE)
    score_scale = HEAD_SIZE ** (-0.5)
    num_c, top_c, tot_c = [
        jnp.concatenate([early, late], axis=0)
        for early, late in zip(attention_early, attention_late)
    ]
    view = (row_dev, local_heads, group_size, HEAD_SIZE)
    flat = (row_dev, local_heads * group_size, HEAD_SIZE)
    query_wide = queries.reshape(view).astype(jnp.float32)
    own_key = new_kv[:, :, :HEAD_SIZE].astype(jnp.float32)[:, :, None, :]
    own_value = jnp.broadcast_to(
        new_kv[:, :, HEAD_SIZE:].astype(jnp.float32)[:, :, None, :], view
    ).reshape(flat)
    own_score = (jnp.sum(query_wide * own_key, axis=-1) * score_scale).reshape(
        row_dev, local_heads * group_size, 1
    )
    cache_weighted = num_c.reshape(flat)
    cache_top = top_c.reshape(flat)
    cache_total = tot_c.reshape(flat)
    score_top = jnp.maximum(cache_top, own_score)
    rescale = jnp.exp(cache_top - score_top)
    own_weight = jnp.exp(own_score - score_top).astype(jnp.bfloat16).astype(jnp.float32)
    weight_total = rescale * cache_total + own_weight
    weighted = rescale * cache_weighted + own_weight * own_value
    attended = (weighted / weight_total).astype(jnp.bfloat16).reshape(row_dev, -1)
    return (hidden_part, new_kv, attended)


def solution(mesh):
    return jax.shard_map(
        per_device,
        mesh=mesh,
        in_specs=(
            P("tensor", "adapter", None),
            P("adapter", None),
            P(),
            P(None, "tensor", None),
            P("tensor", "adapter"),
            P("adapter", "tensor", None),
            P("adapter"),
            P("adapter", "tensor"),
            P("adapter", None, None, "tensor"),
            P("adapter"),
        ),
        out_specs=(P("adapter", "tensor"), P("adapter", "tensor", None), P("adapter", "tensor")),
        check_vma=False,
    )
```

```python
import functools

import jax
import jax.numpy as jnp
from jax import lax
from jax.experimental import pallas as pl
from jax.experimental.pallas import tpu as pltpu
from jax.sharding import PartitionSpec as P

HEAD_SIZE = 128
ADAPTER_RANK = 64
FAN = 8


EPSILON = 1e-05
ADAPTER_SCALE = 0.5
ID_LANES = 128


def _attn_kernel(len_ref, q_ref, k_ref, v_ref, num_ref, top_ref, tot_ref, *, heads, group, scale, first):
    p = pl.program_id(0) + first
    length = len_ref[p]
    fan = q_ref.shape[0]
    head_width = group * HEAD_SIZE
    for k in range(heads):
        lanes = pl.ds(k * HEAD_SIZE, HEAD_SIZE)
        qs = jnp.concatenate(
            [q_ref[:, pl.ds(k * head_width + g * HEAD_SIZE, HEAD_SIZE)] for g in range(group)], axis=0)
        kb = k_ref[0, 0, :, lanes]
        s = lax.dot_general(qs, kb, (((1,), (1,)), ((), ())), preferred_element_type=jnp.float32) * scale
        col = lax.broadcasted_iota(jnp.int32, s.shape, 1)
        s = jnp.where(col < length, s, -jnp.inf)
        m = jnp.max(s, axis=1, keepdims=True)
        w = jnp.exp(s - m).astype(jnp.bfloat16)
        tot = jnp.sum(w.astype(jnp.float32), axis=1, keepdims=True)
        num = jnp.dot(w, v_ref[0, 0, :, lanes], preferred_element_type=jnp.float32)
        for g in range(group):
            out_lanes = pl.ds(k * head_width + g * HEAD_SIZE, HEAD_SIZE)
            rows = slice(g * fan, (g + 1) * fan)
            num_ref[:, out_lanes] = num[rows]
            top_ref[:, out_lanes] = jnp.broadcast_to(m[rows], (fan, HEAD_SIZE))
            tot_ref[:, out_lanes] = jnp.broadcast_to(tot[rows], (fan, HEAD_SIZE))


def cache_attention(queries, key_value_cache, prompt_cache_length, local_heads, fan, first, count):
    _, _, cache_len, kv_width = key_value_cache.shape
    width = queries.shape[1]
    group = width // (local_heads * HEAD_SIZE)
    kernel = functools.partial(
        _attn_kernel, heads=local_heads, group=group, scale=HEAD_SIZE ** (-0.5), first=first)
    out = jax.ShapeDtypeStruct((count * fan, width), jnp.float32)
    spec_out = pl.BlockSpec((fan, width), lambda p, lens: (p, 0))
    return pl.pallas_call(
        kernel,
        out_shape=(out, out, out),
        grid_spec=pltpu.PrefetchScalarGridSpec(
            num_scalar_prefetch=1,
            grid=(count,),
            in_specs=[
                pl.BlockSpec((fan, width), lambda p, lens: (p + first, 0)),
                pl.BlockSpec((1, 1, cache_len, kv_width), lambda p, lens: (p + first, 0, 0, 0)),
                pl.BlockSpec((1, 1, cache_len, kv_width), lambda p, lens: (p + first, 1, 0, 0)),
            ],
            out_specs=[spec_out, spec_out, spec_out],
        ),
        cost_estimate=pl.CostEstimate(
            flops=4 * count * fan * width * cache_len,
            transcendentals=count * fan * width * cache_len // HEAD_SIZE,
            bytes_accessed=count * (2 * cache_len * kv_width * 2 + fan * width * 14),
        ),
    )(prompt_cache_length, queries, key_value_cache, key_value_cache)


def _swap(x, mask, count):
    return lax.ppermute(x, "tensor", perm=[(i, i ^ mask) for i in range(count)])


def per_device(
    partials,
    residual,
    attention_norm_gain,
    key_value_weight,
    adapter_down_weight,
    adapter_up_weight,
    row_adapter_index,
    queries,
    key_value_cache,
    prompt_cache_length,
):
    row_dev = residual.shape[0]
    model_width = residual.shape[1]
    tensor_count = lax.axis_size("tensor")
    quarter = model_width // tensor_count
    tensor_index = lax.axis_index("tensor")
    core = tensor_index % 2
    chip_x = tensor_index // 2
    local_heads = key_value_weight.shape[1]
    head_weight = jnp.transpose(key_value_weight, (1, 0, 2))

    half_rows = row_dev // 2
    part2 = partials[0].reshape(2, half_rows, model_width)
    mine_p = lax.dynamic_index_in_dim(part2, core, axis=0, keepdims=False)
    other_p = lax.dynamic_index_in_dim(part2, 1 - core, axis=0, keepdims=False)
    got_p = _swap(other_p, 1, tensor_count)
    chip_sum = mine_p.astype(jnp.float32) + got_p.astype(jnp.float32)
    far_sum = _swap(chip_sum.astype(jnp.bfloat16), 2, tensor_count)
    local_prompts = key_value_cache.shape[0]
    early_prompts = local_prompts // 2
    attention_early = cache_attention(
        queries, key_value_cache, prompt_cache_length, local_heads, FAN, 0, early_prompts
    )
    far_sum, head_weight, attention_early = lax.optimization_barrier(
        (far_sum, head_weight, attention_early)
    )
    res_half = lax.dynamic_index_in_dim(
        residual.reshape(2, half_rows, model_width), core, axis=0, keepdims=False
    )
    hidden_half = (
        res_half.astype(jnp.float32) + (chip_sum + far_sum.astype(jnp.float32))
    ).astype(jnp.bfloat16)
    hidden_wide = hidden_half.astype(jnp.float32)
    mean_sq = jnp.mean(hidden_wide * hidden_wide, axis=1, keepdims=True)
    normed_half = (
        hidden_wide * lax.rsqrt(mean_sq + EPSILON) * attention_norm_gain.astype(jnp.float32)
    ).astype(jnp.bfloat16)
    partner_cols = (tensor_index ^ 1) * quarter
    to_partner = jnp.concatenate(
        [
            lax.dynamic_slice_in_dim(normed_half, partner_cols, quarter, 1),
            lax.dynamic_slice_in_dim(hidden_half, partner_cols, quarter, 1),
        ],
        axis=1,
    )
    from_partner = _swap(to_partner, 1, tensor_count)
    normed_other_full = _swap(normed_half, 1, tensor_count)
    own_cols = tensor_index * quarter
    normed_mine = lax.dynamic_slice_in_dim(normed_half, own_cols, quarter, 1)
    hidden_mine = lax.dynamic_slice_in_dim(hidden_half, own_cols, quarter, 1)
    normed_other = from_partner[:, :quarter]
    hidden_other = from_partner[:, quarter:]

    first = core == 0

    def by_core(mine, other):
        return jnp.where(
            first,
            jnp.concatenate([mine, other], axis=0),
            jnp.concatenate([other, mine], axis=0),
        )

    hidden_part = by_core(hidden_mine, hidden_other)
    normed_part = by_core(normed_mine, normed_other)
    normed_full = by_core(normed_half, normed_other_full)
    base_kv = jnp.einsum(
        "rf,hfd->rhd", normed_full, head_weight, preferred_element_type=jnp.float32
    ).reshape(row_dev, -1)

    adapt_count = lax.axis_size("adapter")
    capacity = max(2, 4 * row_dev // adapt_count)
    slot_count = adapt_count * capacity
    adapter_grouped = adapter_down_weight.shape[1] // ADAPTER_RANK
    owner_index = row_adapter_index // adapter_grouped
    local_id = row_adapter_index % adapter_grouped
    row_order = jnp.arange(row_dev)
    same_owner = owner_index[:, None] == owner_index[None, :]
    earlier = row_order[None, :] < row_order[:, None]
    slot_rank = jnp.sum((same_owner & earlier).astype(jnp.int32), axis=1)
    row_slot = owner_index * capacity + slot_rank
    row_to_slot = jnp.arange(slot_count)[:, None] == row_slot[None, :]
    slot_matrix = row_to_slot.astype(jnp.bfloat16)
    id_block = jnp.broadcast_to(
        (local_id + 1).astype(jnp.bfloat16)[:, None], (row_dev, ID_LANES)
    )
    payload = (
        jnp.dot(
            slot_matrix,
            jnp.concatenate([normed_part, id_block], axis=1),
            preferred_element_type=jnp.float32,
        )
        .astype(jnp.bfloat16)
        .reshape(adapt_count, capacity, quarter + ID_LANES)
    )
    flattened_up = adapter_up_weight.reshape(adapter_grouped * ADAPTER_RANK, -1)
    payload, queries_late = lax.optimization_barrier((payload, queries))
    rows_in = lax.all_to_all(payload, "adapter", split_axis=0, concat_axis=0, tiled=True)
    attention_late = cache_attention(
        queries_late,
        key_value_cache,
        prompt_cache_length,
        local_heads,
        FAN,
        early_prompts,
        local_prompts - early_prompts,
    )
    rows_in, base_kv, attention_late = lax.optimization_barrier(
        (rows_in, base_kv, attention_late)
    )
    item_count = rows_in.shape[1]
    rows_in = rows_in.reshape(slot_count, quarter + ID_LANES)
    flattened_rows = rows_in[:, :quarter]
    ids_in = rows_in[:, quarter].astype(jnp.int32) - 1
    adapter_pick = ids_in[:, None] == jnp.arange(adapter_grouped)[None, :]
    projected_rows = jnp.dot(
        flattened_rows, adapter_down_weight, preferred_element_type=jnp.float32
    ).reshape(-1, adapter_grouped, ADAPTER_RANK)
    partial_low = jnp.sum(jnp.where(adapter_pick[:, :, None], projected_rows, 0.0), axis=1)
    low_core = _swap(partial_low, 1, tensor_count)
    low_chip = _swap(partial_low, 2, tensor_count)
    low_diag = _swap(partial_low, 3, tensor_count)
    reduced_rank_rows = ((partial_low + low_core) + (low_chip + low_diag)).astype(jnp.bfloat16)
    expanded_rows = jnp.where(
        adapter_pick[:, :, None], reduced_rank_rows[:, None, :], jnp.zeros((), jnp.bfloat16)
    ).reshape(-1, adapter_grouped * ADAPTER_RANK)
    adapter_update = (
        ADAPTER_SCALE * jnp.dot(expanded_rows, flattened_up, preferred_element_type=jnp.float32)
    ).astype(jnp.bfloat16)
    adapter_update = adapter_update.reshape(adapt_count, item_count, -1)
    returned = lax.all_to_all(adapter_update, "adapter", split_axis=0, concat_axis=0, tiled=True)
    returned = returned.reshape(slot_count, -1)
    update_rows = lax.dot_general(
        slot_matrix, returned, (((0,), (0,)), ((), ())), preferred_element_type=jnp.float32
    )
    new_kv = (
        (base_kv + update_rows).astype(jnp.bfloat16).reshape(row_dev, local_heads, 2 * HEAD_SIZE)
    )

    group_size = queries.shape[1] // (local_heads * HEAD_SIZE)
    score_scale = HEAD_SIZE ** (-0.5)
    num_c, top_c, tot_c = [
        jnp.concatenate([early, late], axis=0)
        for early, late in zip(attention_early, attention_late)
    ]
    view = (row_dev, local_heads, group_size, HEAD_SIZE)
    flat = (row_dev, local_heads * group_size, HEAD_SIZE)
    query_wide = queries.reshape(view).astype(jnp.float32)
    own_key = new_kv[:, :, :HEAD_SIZE].astype(jnp.float32)[:, :, None, :]
    own_value = jnp.broadcast_to(
        new_kv[:, :, HEAD_SIZE:].astype(jnp.float32)[:, :, None, :], view
    ).reshape(flat)
    own_score = (jnp.sum(query_wide * own_key, axis=-1) * score_scale).reshape(
        row_dev, local_heads * group_size, 1
    )
    cache_weighted = num_c.reshape(flat)
    cache_top = top_c.reshape(flat)
    cache_total = tot_c.reshape(flat)
    score_top = jnp.maximum(cache_top, own_score)
    rescale = jnp.exp(cache_top - score_top)
    own_weight = jnp.exp(own_score - score_top).astype(jnp.bfloat16).astype(jnp.float32)
    weight_total = rescale * cache_total + own_weight
    weighted = rescale * cache_weighted + own_weight * own_value
    attended = (weighted / weight_total).astype(jnp.bfloat16).reshape(row_dev, -1)
    return (hidden_part, new_kv, attended)


def solution(mesh):
    return jax.shard_map(
        per_device,
        mesh=mesh,
        in_specs=(
            P("tensor", "adapter", None),
            P("adapter", None),
            P(),
            P(None, "tensor", None),
            P("tensor", "adapter"),
            P("adapter", "tensor", None),
            P("adapter"),
            P("adapter", "tensor"),
            P("adapter", None, None, "tensor"),
            P("adapter"),
        ),
        out_specs=(P("adapter", "tensor"), P("adapter", "tensor", None), P("adapter", "tensor")),
        check_vma=False,
    )
```

```python
import functools

import jax
import jax.numpy as jnp
from jax import lax
from jax.experimental import pallas as pl
from jax.experimental.pallas import tpu as pltpu
from jax.sharding import PartitionSpec as P

HEAD_SIZE = 128
ADAPTER_RANK = 64
FAN = 8


EPSILON = 1e-05
ADAPTER_SCALE = 0.5
ID_LANES = 128


def _attn_kernel(len_ref, q_ref, k_ref, v_ref, num_ref, top_ref, tot_ref, *, heads, group, scale, first):
    p = pl.program_id(0) + first
    length = len_ref[p]
    fan = q_ref.shape[0]
    head_width = group * HEAD_SIZE
    for k in range(heads):
        lanes = pl.ds(k * HEAD_SIZE, HEAD_SIZE)
        qs = jnp.concatenate(
            [q_ref[:, pl.ds(k * head_width + g * HEAD_SIZE, HEAD_SIZE)] for g in range(group)], axis=0)
        kb = k_ref[0, 0, :, lanes]
        s = lax.dot_general(qs, kb, (((1,), (1,)), ((), ())), preferred_element_type=jnp.float32) * scale
        col = lax.broadcasted_iota(jnp.int32, s.shape, 1)
        s = jnp.where(col < length, s, -jnp.inf)
        m = jnp.max(s, axis=1, keepdims=True)
        w = jnp.exp(s - m).astype(jnp.bfloat16)
        tot = jnp.sum(w.astype(jnp.float32), axis=1, keepdims=True)
        num = jnp.dot(w, v_ref[0, 0, :, lanes], preferred_element_type=jnp.float32)
        for g in range(group):
            out_lanes = pl.ds(k * head_width + g * HEAD_SIZE, HEAD_SIZE)
            rows = slice(g * fan, (g + 1) * fan)
            num_ref[:, out_lanes] = num[rows]
            top_ref[:, out_lanes] = jnp.broadcast_to(m[rows], (fan, HEAD_SIZE))
            tot_ref[:, out_lanes] = jnp.broadcast_to(tot[rows], (fan, HEAD_SIZE))


def cache_attention(queries, key_value_cache, prompt_cache_length, local_heads, fan, first, count):
    _, _, cache_len, kv_width = key_value_cache.shape
    width = queries.shape[1]
    group = width // (local_heads * HEAD_SIZE)
    kernel = functools.partial(
        _attn_kernel, heads=local_heads, group=group, scale=HEAD_SIZE ** (-0.5), first=first)
    out = jax.ShapeDtypeStruct((count * fan, width), jnp.float32)
    spec_out = pl.BlockSpec((fan, width), lambda p, lens: (p, 0))
    return pl.pallas_call(
        kernel,
        out_shape=(out, out, out),
        grid_spec=pltpu.PrefetchScalarGridSpec(
            num_scalar_prefetch=1,
            grid=(count,),
            in_specs=[
                pl.BlockSpec((fan, width), lambda p, lens: (p + first, 0)),
                pl.BlockSpec((1, 1, cache_len, kv_width), lambda p, lens: (p + first, 0, 0, 0)),
                pl.BlockSpec((1, 1, cache_len, kv_width), lambda p, lens: (p + first, 1, 0, 0)),
            ],
            out_specs=[spec_out, spec_out, spec_out],
        ),
        cost_estimate=pl.CostEstimate(
            flops=4 * count * fan * width * cache_len,
            transcendentals=count * fan * width * cache_len // HEAD_SIZE,
            bytes_accessed=count * (2 * cache_len * kv_width * 2 + fan * width * 14),
        ),
    )(prompt_cache_length, queries, key_value_cache, key_value_cache)


def _swap(x, mask, count):
    return lax.ppermute(x, "tensor", perm=[(i, i ^ mask) for i in range(count)])


def per_device(
    partials,
    residual,
    attention_norm_gain,
    key_value_weight,
    adapter_down_weight,
    adapter_up_weight,
    row_adapter_index,
    queries,
    key_value_cache,
    prompt_cache_length,
):
    row_dev = residual.shape[0]
    model_width = residual.shape[1]
    tensor_count = lax.axis_size("tensor")
    quarter = model_width // tensor_count
    tensor_index = lax.axis_index("tensor")
    core = tensor_index % 2
    chip_x = tensor_index // 2
    local_heads = key_value_weight.shape[1]
    head_weight = jnp.transpose(key_value_weight, (1, 0, 2))

    half_rows = row_dev // 2
    part2 = partials[0].reshape(2, half_rows, model_width)
    mine_p = lax.dynamic_index_in_dim(part2, core, axis=0, keepdims=False)
    other_p = lax.dynamic_index_in_dim(part2, 1 - core, axis=0, keepdims=False)
    got_p = _swap(other_p, 1, tensor_count)
    chip_sum = mine_p.astype(jnp.float32) + got_p.astype(jnp.float32)
    far_sum = _swap(chip_sum.astype(jnp.bfloat16), 2, tensor_count)
    local_prompts = key_value_cache.shape[0]
    early_prompts = local_prompts // 2
    attention_early = cache_attention(
        queries, key_value_cache, prompt_cache_length, local_heads, FAN, 0, early_prompts
    )
    far_sum, head_weight, attention_early = lax.optimization_barrier(
        (far_sum, head_weight, attention_early)
    )
    res_half = lax.dynamic_index_in_dim(
        residual.reshape(2, half_rows, model_width), core, axis=0, keepdims=False
    )
    hidden_half = (
        res_half.astype(jnp.float32) + (chip_sum + far_sum.astype(jnp.float32))
    ).astype(jnp.bfloat16)
    hidden_wide = hidden_half.astype(jnp.float32)
    mean_sq = jnp.mean(hidden_wide * hidden_wide, axis=1, keepdims=True)
    normed_half = (
        hidden_wide * lax.rsqrt(mean_sq + EPSILON) * attention_norm_gain.astype(jnp.float32)
    ).astype(jnp.bfloat16)
    partner_cols = (tensor_index ^ 1) * quarter
    to_partner = jnp.concatenate(
        [
            lax.dynamic_slice_in_dim(normed_half, partner_cols, quarter, 1),
            lax.dynamic_slice_in_dim(hidden_half, partner_cols, quarter, 1),
        ],
        axis=1,
    )
    from_partner = _swap(to_partner, 1, tensor_count)
    normed_other_full = _swap(normed_half, 1, tensor_count)
    own_cols = tensor_index * quarter
    normed_mine = lax.dynamic_slice_in_dim(normed_half, own_cols, quarter, 1)
    hidden_mine = lax.dynamic_slice_in_dim(hidden_half, own_cols, quarter, 1)
    normed_other = from_partner[:, :quarter]
    hidden_other = from_partner[:, quarter:]

    first = core == 0

    def by_core(mine, other):
        return jnp.where(
            first,
            jnp.concatenate([mine, other], axis=0),
            jnp.concatenate([other, mine], axis=0),
        )

    hidden_part = by_core(hidden_mine, hidden_other)
    normed_part = by_core(normed_mine, normed_other)
    normed_full = by_core(normed_half, normed_other_full)
    base_kv = jnp.einsum(
        "rf,hfd->rhd", normed_full, head_weight, preferred_element_type=jnp.float32
    ).reshape(row_dev, -1)

    adapt_count = lax.axis_size("adapter")
    capacity = max(2, 4 * row_dev // adapt_count)
    slot_count = adapt_count * capacity
    adapter_grouped = adapter_down_weight.shape[1] // ADAPTER_RANK
    owner_index = row_adapter_index // adapter_grouped
    local_id = row_adapter_index % adapter_grouped
    row_order = jnp.arange(row_dev)
    same_owner = owner_index[:, None] == owner_index[None, :]
    earlier = row_order[None, :] < row_order[:, None]
    slot_rank = jnp.sum((same_owner & earlier).astype(jnp.int32), axis=1)
    row_slot = owner_index * capacity + slot_rank
    row_to_slot = jnp.arange(slot_count)[:, None] == row_slot[None, :]
    slot_matrix = row_to_slot.astype(jnp.bfloat16)
    id_block = jnp.broadcast_to(
        (local_id + 1).astype(jnp.bfloat16)[:, None], (row_dev, ID_LANES)
    )
    payload = (
        jnp.dot(
            slot_matrix,
            jnp.concatenate([normed_part, id_block], axis=1),
            preferred_element_type=jnp.float32,
        )
        .astype(jnp.bfloat16)
        .reshape(adapt_count, capacity, quarter + ID_LANES)
    )
    flattened_up = adapter_up_weight.reshape(adapter_grouped * ADAPTER_RANK, -1)
    rows_in = lax.all_to_all(payload, "adapter", split_axis=0, concat_axis=0, tiled=True)
    rows_in, base_kv = lax.optimization_barrier((rows_in, base_kv))
    item_count = rows_in.shape[1]
    rows_in = rows_in.reshape(slot_count, quarter + ID_LANES)
    flattened_rows = rows_in[:, :quarter]
    ids_in = rows_in[:, quarter].astype(jnp.int32) - 1
    adapter_pick = ids_in[:, None] == jnp.arange(adapter_grouped)[None, :]
    projected_rows = jnp.dot(
        flattened_rows, adapter_down_weight, preferred_element_type=jnp.float32
    ).reshape(-1, adapter_grouped, ADAPTER_RANK)
    partial_low = jnp.sum(jnp.where(adapter_pick[:, :, None], projected_rows, 0.0), axis=1)
    low_core = _swap(partial_low, 1, tensor_count)
    low_chip = _swap(partial_low, 2, tensor_count)
    low_diag = _swap(partial_low, 3, tensor_count)
    reduced_rank_rows = ((partial_low + low_core) + (low_chip + low_diag)).astype(jnp.bfloat16)
    expanded_rows = jnp.where(
        adapter_pick[:, :, None], reduced_rank_rows[:, None, :], jnp.zeros((), jnp.bfloat16)
    ).reshape(-1, adapter_grouped * ADAPTER_RANK)
    adapter_update = (
        ADAPTER_SCALE * jnp.dot(expanded_rows, flattened_up, preferred_element_type=jnp.float32)
    ).astype(jnp.bfloat16)
    adapter_update = adapter_update.reshape(adapt_count, item_count, -1)
    adapter_update, queries_late = lax.optimization_barrier((adapter_update, queries))
    returned = lax.all_to_all(adapter_update, "adapter", split_axis=0, concat_axis=0, tiled=True)
    attention_late = cache_attention(
        queries_late,
        key_value_cache,
        prompt_cache_length,
        local_heads,
        FAN,
        early_prompts,
        local_prompts - early_prompts,
    )
    returned, attention_late = lax.optimization_barrier((returned, attention_late))
    returned = returned.reshape(slot_count, -1)
    update_rows = lax.dot_general(
        slot_matrix, returned, (((0,), (0,)), ((), ())), preferred_element_type=jnp.float32
    )
    new_kv = (
        (base_kv + update_rows).astype(jnp.bfloat16).reshape(row_dev, local_heads, 2 * HEAD_SIZE)
    )

    group_size = queries.shape[1] // (local_heads * HEAD_SIZE)
    score_scale = HEAD_SIZE ** (-0.5)
    num_c, top_c, tot_c = [
        jnp.concatenate([early, late], axis=0)
        for early, late in zip(attention_early, attention_late)
    ]
    view = (row_dev, local_heads, group_size, HEAD_SIZE)
    flat = (row_dev, local_heads * group_size, HEAD_SIZE)
    query_wide = queries.reshape(view).astype(jnp.float32)
    own_key = new_kv[:, :, :HEAD_SIZE].astype(jnp.float32)[:, :, None, :]
    own_value = jnp.broadcast_to(
        new_kv[:, :, HEAD_SIZE:].astype(jnp.float32)[:, :, None, :], view
    ).reshape(flat)
    own_score = (jnp.sum(query_wide * own_key, axis=-1) * score_scale).reshape(
        row_dev, local_heads * group_size, 1
    )
    cache_weighted = num_c.reshape(flat)
    cache_top = top_c.reshape(flat)
    cache_total = tot_c.reshape(flat)
    score_top = jnp.maximum(cache_top, own_score)
    rescale = jnp.exp(cache_top - score_top)
    own_weight = jnp.exp(own_score - score_top).astype(jnp.bfloat16).astype(jnp.float32)
    weight_total = rescale * cache_total + own_weight
    weighted = rescale * cache_weighted + own_weight * own_value
    attended = (weighted / weight_total).astype(jnp.bfloat16).reshape(row_dev, -1)
    return (hidden_part, new_kv, attended)


def solution(mesh):
    return jax.shard_map(
        per_device,
        mesh=mesh,
        in_specs=(
            P("tensor", "adapter", None),
            P("adapter", None),
            P(),
            P(None, "tensor", None),
            P("tensor", "adapter"),
            P("adapter", "tensor", None),
            P("adapter"),
            P("adapter", "tensor"),
            P("adapter", None, None, "tensor"),
            P("adapter"),
        ),
        out_specs=(P("adapter", "tensor"), P("adapter", "tensor", None), P("adapter", "tensor")),
        check_vma=False,
    )
```

```python
import functools

import jax
import jax.numpy as jnp
from jax import lax
from jax.experimental import pallas as pl
from jax.experimental.pallas import tpu as pltpu
from jax.sharding import PartitionSpec as P

HEAD_SIZE = 128
ADAPTER_RANK = 64
FAN = 8


EPSILON = 1e-05
ADAPTER_SCALE = 0.5
ID_LANES = 128


def _attn_kernel(len_ref, q_ref, k_ref, v_ref, num_ref, top_ref, tot_ref, *, heads, group, scale, first):
    p = pl.program_id(0) + first
    length = len_ref[p]
    fan = q_ref.shape[0]
    head_width = group * HEAD_SIZE
    for k in range(heads):
        lanes = pl.ds(k * HEAD_SIZE, HEAD_SIZE)
        qs = jnp.concatenate(
            [q_ref[:, pl.ds(k * head_width + g * HEAD_SIZE, HEAD_SIZE)] for g in range(group)], axis=0)
        kb = k_ref[0, 0, :, lanes]
        s = lax.dot_general(qs, kb, (((1,), (1,)), ((), ())), preferred_element_type=jnp.float32) * scale
        col = lax.broadcasted_iota(jnp.int32, s.shape, 1)
        s = jnp.where(col < length, s, -jnp.inf)
        m = jnp.max(s, axis=1, keepdims=True)
        w = jnp.exp(s - m).astype(jnp.bfloat16)
        tot = jnp.sum(w.astype(jnp.float32), axis=1, keepdims=True)
        num = jnp.dot(w, v_ref[0, 0, :, lanes], preferred_element_type=jnp.float32)
        for g in range(group):
            out_lanes = pl.ds(k * head_width + g * HEAD_SIZE, HEAD_SIZE)
            rows = slice(g * fan, (g + 1) * fan)
            num_ref[:, out_lanes] = num[rows]
            top_ref[:, out_lanes] = jnp.broadcast_to(m[rows], (fan, HEAD_SIZE))
            tot_ref[:, out_lanes] = jnp.broadcast_to(tot[rows], (fan, HEAD_SIZE))


def cache_attention(queries, key_value_cache, prompt_cache_length, local_heads, fan, first, count):
    _, _, cache_len, kv_width = key_value_cache.shape
    width = queries.shape[1]
    group = width // (local_heads * HEAD_SIZE)
    kernel = functools.partial(
        _attn_kernel, heads=local_heads, group=group, scale=HEAD_SIZE ** (-0.5), first=first)
    out = jax.ShapeDtypeStruct((count * fan, width), jnp.float32)
    spec_out = pl.BlockSpec((fan, width), lambda p, lens: (p, 0))
    return pl.pallas_call(
        kernel,
        out_shape=(out, out, out),
        grid_spec=pltpu.PrefetchScalarGridSpec(
            num_scalar_prefetch=1,
            grid=(count,),
            in_specs=[
                pl.BlockSpec((fan, width), lambda p, lens: (p + first, 0)),
                pl.BlockSpec((1, 1, cache_len, kv_width), lambda p, lens: (p + first, 0, 0, 0)),
                pl.BlockSpec((1, 1, cache_len, kv_width), lambda p, lens: (p + first, 1, 0, 0)),
            ],
            out_specs=[spec_out, spec_out, spec_out],
        ),
        cost_estimate=pl.CostEstimate(
            flops=4 * count * fan * width * cache_len,
            transcendentals=count * fan * width * cache_len // HEAD_SIZE,
            bytes_accessed=count * (2 * cache_len * kv_width * 2 + fan * width * 14),
        ),
    )(prompt_cache_length, queries, key_value_cache, key_value_cache)


def _swap(x, mask, count):
    return lax.ppermute(x, "tensor", perm=[(i, i ^ mask) for i in range(count)])


def per_device(
    partials,
    residual,
    attention_norm_gain,
    key_value_weight,
    adapter_down_weight,
    adapter_up_weight,
    row_adapter_index,
    queries,
    key_value_cache,
    prompt_cache_length,
):
    row_dev = residual.shape[0]
    model_width = residual.shape[1]
    tensor_count = lax.axis_size("tensor")
    quarter = model_width // tensor_count
    tensor_index = lax.axis_index("tensor")
    core = tensor_index % 2
    chip_x = tensor_index // 2
    local_heads = key_value_weight.shape[1]
    head_weight = jnp.transpose(key_value_weight, (1, 0, 2))

    half_rows = row_dev // 2
    part2 = partials[0].reshape(2, half_rows, model_width)
    mine_p = lax.dynamic_index_in_dim(part2, core, axis=0, keepdims=False)
    other_p = lax.dynamic_index_in_dim(part2, 1 - core, axis=0, keepdims=False)
    got_p = _swap(other_p, 1, tensor_count)
    chip_sum = mine_p.astype(jnp.float32) + got_p.astype(jnp.float32)
    far_sum = _swap(chip_sum.astype(jnp.bfloat16), 2, tensor_count)
    local_prompts = key_value_cache.shape[0]
    early_prompts = local_prompts // 2
    attention_early = cache_attention(
        queries, key_value_cache, prompt_cache_length, local_heads, FAN, 0, early_prompts
    )
    far_sum, head_weight, attention_early = lax.optimization_barrier(
        (far_sum, head_weight, attention_early)
    )
    res_half = lax.dynamic_index_in_dim(
        residual.reshape(2, half_rows, model_width), core, axis=0, keepdims=False
    )
    hidden_half = (
        res_half.astype(jnp.float32) + (chip_sum + far_sum.astype(jnp.float32))
    ).astype(jnp.bfloat16)
    hidden_wide = hidden_half.astype(jnp.float32)
    mean_sq = jnp.mean(hidden_wide * hidden_wide, axis=1, keepdims=True)
    normed_half = (
        hidden_wide * lax.rsqrt(mean_sq + EPSILON) * attention_norm_gain.astype(jnp.float32)
    ).astype(jnp.bfloat16)
    partner_cols = (tensor_index ^ 1) * quarter
    to_partner = jnp.concatenate(
        [
            lax.dynamic_slice_in_dim(normed_half, partner_cols, quarter, 1),
            lax.dynamic_slice_in_dim(hidden_half, partner_cols, quarter, 1),
        ],
        axis=1,
    )
    from_partner = _swap(to_partner, 1, tensor_count)
    normed_other_full = _swap(normed_half, 1, tensor_count)
    own_cols = tensor_index * quarter
    normed_mine = lax.dynamic_slice_in_dim(normed_half, own_cols, quarter, 1)
    hidden_mine = lax.dynamic_slice_in_dim(hidden_half, own_cols, quarter, 1)
    normed_other = from_partner[:, :quarter]
    hidden_other = from_partner[:, quarter:]
    first = core == 0

    def by_core(mine, other):
        return jnp.where(
            first,
            jnp.concatenate([mine, other], axis=0),
            jnp.concatenate([other, mine], axis=0),
        )

    hidden_part = by_core(hidden_mine, hidden_other)
    normed_part = by_core(normed_mine, normed_other)
    normed_full = by_core(normed_half, normed_other_full)
    base_kv = jnp.einsum(
        "rf,hfd->rhd", normed_full, head_weight, preferred_element_type=jnp.float32
    ).reshape(row_dev, -1)

    adapt_count = lax.axis_size("adapter")
    capacity = max(2, 4 * row_dev // adapt_count)
    slot_count = adapt_count * capacity
    adapter_grouped = adapter_down_weight.shape[1] // ADAPTER_RANK
    owner_index = row_adapter_index // adapter_grouped
    local_id = row_adapter_index % adapter_grouped
    row_order = jnp.arange(row_dev)
    same_owner = owner_index[:, None] == owner_index[None, :]
    earlier = row_order[None, :] < row_order[:, None]
    slot_rank = jnp.sum((same_owner & earlier).astype(jnp.int32), axis=1)
    row_slot = owner_index * capacity + slot_rank
    row_to_slot = jnp.arange(slot_count)[:, None] == row_slot[None, :]
    slot_matrix = row_to_slot.astype(jnp.bfloat16)
    id_block = jnp.broadcast_to(
        (local_id + 1).astype(jnp.bfloat16)[:, None], (row_dev, ID_LANES)
    )
    payload = (
        jnp.dot(
            slot_matrix,
            jnp.concatenate([normed_part, id_block], axis=1),
            preferred_element_type=jnp.float32,
        )
        .astype(jnp.bfloat16)
        .reshape(adapt_count, capacity, quarter + ID_LANES)
    )
    flattened_up = adapter_up_weight.reshape(adapter_grouped * ADAPTER_RANK, -1)
    rows_in = lax.all_to_all(payload, "adapter", split_axis=0, concat_axis=0, tiled=True)
    item_count = rows_in.shape[1]
    rows_in = rows_in.reshape(slot_count, quarter + ID_LANES)
    flattened_rows = rows_in[:, :quarter]
    ids_in = rows_in[:, quarter].astype(jnp.int32) - 1
    adapter_pick = ids_in[:, None] == jnp.arange(adapter_grouped)[None, :]
    projected_rows = jnp.dot(
        flattened_rows, adapter_down_weight, preferred_element_type=jnp.float32
    ).reshape(-1, adapter_grouped, ADAPTER_RANK)
    partial_low = jnp.sum(jnp.where(adapter_pick[:, :, None], projected_rows, 0.0), axis=1)
    pair_low = partial_low + _swap(partial_low, 1, tensor_count)
    far_low, base_kv = lax.optimization_barrier((_swap(pair_low, 2, tensor_count), base_kv))
    reduced_rank_rows = (pair_low + far_low).astype(jnp.bfloat16)
    expanded_rows = jnp.where(
        adapter_pick[:, :, None], reduced_rank_rows[:, None, :], jnp.zeros((), jnp.bfloat16)
    ).reshape(-1, adapter_grouped * ADAPTER_RANK)
    adapter_update = (
        ADAPTER_SCALE * jnp.dot(expanded_rows, flattened_up, preferred_element_type=jnp.float32)
    ).astype(jnp.bfloat16)
    adapter_update = adapter_update.reshape(adapt_count, item_count, -1)
    returned = lax.all_to_all(adapter_update, "adapter", split_axis=0, concat_axis=0, tiled=True)
    attention_late = cache_attention(
        queries,
        key_value_cache,
        prompt_cache_length,
        local_heads,
        FAN,
        early_prompts,
        local_prompts - early_prompts,
    )
    returned, attention_late = lax.optimization_barrier((returned, attention_late))
    returned = returned.reshape(slot_count, -1)
    update_rows = lax.dot_general(
        slot_matrix, returned, (((0,), (0,)), ((), ())), preferred_element_type=jnp.float32
    )
    new_kv = (
        (base_kv + update_rows).astype(jnp.bfloat16).reshape(row_dev, local_heads, 2 * HEAD_SIZE)
    )

    group_size = queries.shape[1] // (local_heads * HEAD_SIZE)
    score_scale = HEAD_SIZE ** (-0.5)
    num_c, top_c, tot_c = [
        jnp.concatenate([early, late], axis=0)
        for early, late in zip(attention_early, attention_late)
    ]
    view = (row_dev, local_heads, group_size, HEAD_SIZE)
    cache_weighted = num_c.reshape(view)
    cache_top = top_c.reshape(view)[..., 0]
    cache_total = tot_c.reshape(view)[..., 0]
    query_heads = queries.reshape(view)
    own_key = new_kv[:, :, :HEAD_SIZE]
    own_value = new_kv[:, :, HEAD_SIZE:]
    own_score = (
        jnp.einsum("rkgd,rkd->rkg", query_heads, own_key, preferred_element_type=jnp.float32)
        * score_scale
    )
    score_top = jnp.maximum(cache_top, own_score)
    rescale = jnp.exp(cache_top - score_top)
    own_weight = jnp.exp(own_score - score_top).astype(jnp.bfloat16).astype(jnp.float32)
    weight_total = rescale * cache_total + own_weight
    weighted = (
        rescale[..., None] * cache_weighted
        + own_weight[..., None] * own_value.astype(jnp.float32)[:, :, None, :]
    )
    attended = (weighted / weight_total[..., None]).astype(jnp.bfloat16).reshape(row_dev, -1)
    return (hidden_part, new_kv, attended)


def solution(mesh):
    return jax.shard_map(
        per_device,
        mesh=mesh,
        in_specs=(
            P("tensor", "adapter", None),
            P("adapter", None),
            P(),
            P(None, "tensor", None),
            P("tensor", "adapter"),
            P("adapter", "tensor", None),
            P("adapter"),
            P("adapter", "tensor"),
            P("adapter", None, None, "tensor"),
            P("adapter"),
        ),
        out_specs=(P("adapter", "tensor"), P("adapter", "tensor", None), P("adapter", "tensor")),
        check_vma=False,
    )
```

```python
import functools

import jax
import jax.numpy as jnp
from jax import lax
from jax.experimental import pallas as pl
from jax.experimental.pallas import tpu as pltpu
from jax.sharding import PartitionSpec as P

HEAD_SIZE = 128
ADAPTER_RANK = 64
FAN = 8


EPSILON = 1e-05
ADAPTER_SCALE = 0.5
ID_LANES = 128


def _attn_kernel(len_ref, q_ref, k_ref, v_ref, num_ref, top_ref, tot_ref, *, heads, group, scale, first):
    p = pl.program_id(0) + first
    length = len_ref[p]
    fan = q_ref.shape[0]
    head_width = group * HEAD_SIZE
    for k in range(heads):
        lanes = pl.ds(k * HEAD_SIZE, HEAD_SIZE)
        qs = jnp.concatenate(
            [q_ref[:, pl.ds(k * head_width + g * HEAD_SIZE, HEAD_SIZE)] for g in range(group)], axis=0)
        kb = k_ref[0, 0, :, lanes]
        s = lax.dot_general(qs, kb, (((1,), (1,)), ((), ())), preferred_element_type=jnp.float32) * scale
        col = lax.broadcasted_iota(jnp.int32, s.shape, 1)
        s = jnp.where(col < length, s, -jnp.inf)
        m = jnp.max(s, axis=1, keepdims=True)
        w = jnp.exp(s - m).astype(jnp.bfloat16)
        tot = jnp.sum(w.astype(jnp.float32), axis=1, keepdims=True)
        num = jnp.dot(w, v_ref[0, 0, :, lanes], preferred_element_type=jnp.float32)
        for g in range(group):
            out_lanes = pl.ds(k * head_width + g * HEAD_SIZE, HEAD_SIZE)
            rows = slice(g * fan, (g + 1) * fan)
            num_ref[:, out_lanes] = num[rows]
            top_ref[:, out_lanes] = jnp.broadcast_to(m[rows], (fan, HEAD_SIZE))
            tot_ref[:, out_lanes] = jnp.broadcast_to(tot[rows], (fan, HEAD_SIZE))


def cache_attention(queries, key_value_cache, prompt_cache_length, local_heads, fan, first, count):
    _, _, cache_len, kv_width = key_value_cache.shape
    width = queries.shape[1]
    group = width // (local_heads * HEAD_SIZE)
    kernel = functools.partial(
        _attn_kernel, heads=local_heads, group=group, scale=HEAD_SIZE ** (-0.5), first=first)
    out = jax.ShapeDtypeStruct((count * fan, width), jnp.float32)
    spec_out = pl.BlockSpec((fan, width), lambda p, lens: (p, 0))
    return pl.pallas_call(
        kernel,
        out_shape=(out, out, out),
        grid_spec=pltpu.PrefetchScalarGridSpec(
            num_scalar_prefetch=1,
            grid=(count,),
            in_specs=[
                pl.BlockSpec((fan, width), lambda p, lens: (p + first, 0)),
                pl.BlockSpec((1, 1, cache_len, kv_width), lambda p, lens: (p + first, 0, 0, 0)),
                pl.BlockSpec((1, 1, cache_len, kv_width), lambda p, lens: (p + first, 1, 0, 0)),
            ],
            out_specs=[spec_out, spec_out, spec_out],
        ),
        cost_estimate=pl.CostEstimate(
            flops=4 * count * fan * width * cache_len,
            transcendentals=count * fan * width * cache_len // HEAD_SIZE,
            bytes_accessed=count * (2 * cache_len * kv_width * 2 + fan * width * 14),
        ),
    )(prompt_cache_length, queries, key_value_cache, key_value_cache)


def _swap(x, mask, count):
    return lax.ppermute(x, "tensor", perm=[(i, i ^ mask) for i in range(count)])


def per_device(
    partials,
    residual,
    attention_norm_gain,
    key_value_weight,
    adapter_down_weight,
    adapter_up_weight,
    row_adapter_index,
    queries,
    key_value_cache,
    prompt_cache_length,
):
    row_dev = residual.shape[0]
    model_width = residual.shape[1]
    tensor_count = lax.axis_size("tensor")
    quarter = model_width // tensor_count
    tensor_index = lax.axis_index("tensor")
    core = tensor_index % 2
    chip_x = tensor_index // 2
    local_heads = key_value_weight.shape[1]
    head_weight = jnp.transpose(key_value_weight, (1, 0, 2))

    half_rows = row_dev // 2
    part2 = partials[0].reshape(2, half_rows, model_width)
    mine_p = lax.dynamic_index_in_dim(part2, core, axis=0, keepdims=False)
    other_p = lax.dynamic_index_in_dim(part2, 1 - core, axis=0, keepdims=False)
    got_p = _swap(other_p, 1, tensor_count)
    chip_sum = mine_p.astype(jnp.float32) + got_p.astype(jnp.float32)
    far_sum = _swap(chip_sum.astype(jnp.bfloat16), 2, tensor_count)
    local_prompts = key_value_cache.shape[0]
    early_prompts = local_prompts // 2
    attention_early = cache_attention(
        queries, key_value_cache, prompt_cache_length, local_heads, FAN, 0, early_prompts
    )
    far_sum, head_weight, attention_early = lax.optimization_barrier(
        (far_sum, head_weight, attention_early)
    )
    res_half = lax.dynamic_index_in_dim(
        residual.reshape(2, half_rows, model_width), core, axis=0, keepdims=False
    )
    hidden_half = (
        res_half.astype(jnp.float32) + (chip_sum + far_sum.astype(jnp.float32))
    ).astype(jnp.bfloat16)
    hidden_wide = hidden_half.astype(jnp.float32)
    mean_sq = jnp.mean(hidden_wide * hidden_wide, axis=1, keepdims=True)
    normed_half = (
        hidden_wide * lax.rsqrt(mean_sq + EPSILON) * attention_norm_gain.astype(jnp.float32)
    ).astype(jnp.bfloat16)
    partner_quarter = lax.dynamic_slice_in_dim(
        hidden_half, (tensor_index ^ 1) * quarter, quarter, 1
    )
    swap_in = _swap(jnp.concatenate([normed_half, partner_quarter], axis=1), 1, tensor_count)
    normed_other = swap_in[:, :model_width]
    hidden_other = swap_in[:, model_width:]
    hidden_mine = lax.dynamic_slice_in_dim(hidden_half, tensor_index * quarter, quarter, 1)
    first = core == 0
    hidden_part = jnp.where(
        first,
        jnp.concatenate([hidden_mine, hidden_other], axis=0),
        jnp.concatenate([hidden_other, hidden_mine], axis=0),
    )
    normed_full = jnp.where(
        first,
        jnp.concatenate([normed_half, normed_other], axis=0),
        jnp.concatenate([normed_other, normed_half], axis=0),
    )
    normed_part = lax.dynamic_slice_in_dim(normed_full, tensor_index * quarter, quarter, 1)
    base_kv = jnp.einsum(
        "rf,hfd->rhd", normed_full, head_weight, preferred_element_type=jnp.float32
    ).reshape(row_dev, -1)

    adapt_count = lax.axis_size("adapter")
    capacity = max(2, 4 * row_dev // adapt_count)
    slot_count = adapt_count * capacity
    adapter_grouped = adapter_down_weight.shape[1] // ADAPTER_RANK
    owner_index = row_adapter_index // adapter_grouped
    local_id = row_adapter_index % adapter_grouped
    row_order = jnp.arange(row_dev)
    same_owner = owner_index[:, None] == owner_index[None, :]
    earlier = row_order[None, :] < row_order[:, None]
    slot_rank = jnp.sum((same_owner & earlier).astype(jnp.int32), axis=1)
    row_slot = owner_index * capacity + slot_rank
    row_to_slot = jnp.arange(slot_count)[:, None] == row_slot[None, :]
    slot_matrix = row_to_slot.astype(jnp.bfloat16)
    id_block = jnp.broadcast_to(
        (local_id + 1).astype(jnp.bfloat16)[:, None], (row_dev, ID_LANES)
    )
    payload = (
        jnp.dot(
            slot_matrix,
            jnp.concatenate([normed_part, id_block], axis=1),
            preferred_element_type=jnp.float32,
        )
        .astype(jnp.bfloat16)
        .reshape(adapt_count, capacity, quarter + ID_LANES)
    )
    flattened_up = adapter_up_weight.reshape(adapter_grouped * ADAPTER_RANK, -1)
    rows_in = lax.all_to_all(payload, "adapter", split_axis=0, concat_axis=0, tiled=True)
    item_count = rows_in.shape[1]
    rows_in = rows_in.reshape(slot_count, quarter + ID_LANES)
    flattened_rows = rows_in[:, :quarter]
    ids_in = rows_in[:, quarter].astype(jnp.int32) - 1
    adapter_pick = ids_in[:, None] == jnp.arange(adapter_grouped)[None, :]
    projected_rows = jnp.dot(
        flattened_rows, adapter_down_weight, preferred_element_type=jnp.float32
    ).reshape(-1, adapter_grouped, ADAPTER_RANK)
    partial_low = jnp.sum(jnp.where(adapter_pick[:, :, None], projected_rows, 0.0), axis=1)
    pair_low = partial_low + _swap(partial_low, 1, tensor_count)
    far_low, base_kv = lax.optimization_barrier((_swap(pair_low, 2, tensor_count), base_kv))
    reduced_rank_rows = (pair_low + far_low).astype(jnp.bfloat16)
    expanded_rows = jnp.where(
        adapter_pick[:, :, None], reduced_rank_rows[:, None, :], jnp.zeros((), jnp.bfloat16)
    ).reshape(-1, adapter_grouped * ADAPTER_RANK)
    adapter_update = (
        ADAPTER_SCALE * jnp.dot(expanded_rows, flattened_up, preferred_element_type=jnp.float32)
    ).astype(jnp.bfloat16)
    adapter_update = adapter_update.reshape(adapt_count, item_count, -1)
    returned = lax.all_to_all(adapter_update, "adapter", split_axis=0, concat_axis=0, tiled=True)
    attention_late = cache_attention(
        queries,
        key_value_cache,
        prompt_cache_length,
        local_heads,
        FAN,
        early_prompts,
        local_prompts - early_prompts,
    )
    returned, attention_late = lax.optimization_barrier((returned, attention_late))
    returned = returned.reshape(slot_count, -1)
    update_rows = lax.dot_general(
        slot_matrix, returned, (((0,), (0,)), ((), ())), preferred_element_type=jnp.float32
    )
    new_kv = (
        (base_kv + update_rows).astype(jnp.bfloat16).reshape(row_dev, local_heads, 2 * HEAD_SIZE)
    )

    group_size = queries.shape[1] // (local_heads * HEAD_SIZE)
    score_scale = HEAD_SIZE ** (-0.5)
    num_c, top_c, tot_c = [
        jnp.concatenate([early, late], axis=0)
        for early, late in zip(attention_early, attention_late)
    ]
    view = (row_dev, local_heads, group_size, HEAD_SIZE)
    cache_weighted = num_c.reshape(view)
    cache_top = top_c.reshape(view)[..., 0]
    cache_total = tot_c.reshape(view)[..., 0]
    query_heads = queries.reshape(view)
    own_key = new_kv[:, :, :HEAD_SIZE]
    own_value = new_kv[:, :, HEAD_SIZE:]
    own_score = (
        jnp.einsum("rkgd,rkd->rkg", query_heads, own_key, preferred_element_type=jnp.float32)
        * score_scale
    )
    score_top = jnp.maximum(cache_top, own_score)
    rescale = jnp.exp(cache_top - score_top)
    own_weight = jnp.exp(own_score - score_top).astype(jnp.bfloat16).astype(jnp.float32)
    weight_total = rescale * cache_total + own_weight
    weighted = (
        rescale[..., None] * cache_weighted
        + own_weight[..., None] * own_value.astype(jnp.float32)[:, :, None, :]
    )
    attended = (weighted / weight_total[..., None]).astype(jnp.bfloat16).reshape(row_dev, -1)
    return (hidden_part, new_kv, attended)


def solution(mesh):
    return jax.shard_map(
        per_device,
        mesh=mesh,
        in_specs=(
            P("tensor", "adapter", None),
            P("adapter", None),
            P(),
            P(None, "tensor", None),
            P("tensor", "adapter"),
            P("adapter", "tensor", None),
            P("adapter"),
            P("adapter", "tensor"),
            P("adapter", None, None, "tensor"),
            P("adapter"),
        ),
        out_specs=(P("adapter", "tensor"), P("adapter", "tensor", None), P("adapter", "tensor")),
        check_vma=False,
    )
```
